32 devices in a mesh: chan: 8 (over z, y), tm: 4 (over x, core).
Axes of the slice: x: 2, y: 2, z: 4, core: 2. Of those that a mesh axis runs over, the one named last changes fastest.
Arguments:
- records: float32 [4, 3200, 512], P('tm', 'chan'), may hold values from -6 to 6
- chan_order: int32 [512], replicated, may hold values from 0 to 511, each once
- live_mask: int32 [512], replicated, may hold values 0 or 1
Outputs:
- stacks: float32 [2, 512, 64, 128], P(None, 'chan', 'tm')
The draws below stay inside these ranges and needn't reach their ends.
Inputs may be any that keep to these rules, and one draw needn't show every extreme that they name: chan_order holds every channel number once.
All inputs are finite; a program needn't handle non-finite values.
Results may differ from the reference program's by a relative error of at most 0.0041.
Values may be sent and summed in bfloat16 or wider, within the bound.
No kernel may reach another device: no remote copies, remote signals or barrier semaphores. Data moves between devices by JAX's collectives and lax.ppermute only.
A program may use at most 64 MiB of HBM per device.

```python
import math
import jax
import jax.numpy as jnp
from jax import lax

L = 200
FB = 101
NLAG = 128
ROUNDS = 2
WIN_TM = 16
CH_DEV = 64
CH = 512
TSUB = 3200
N_CHAN = 8
N_TM = 4


def plant(drawn, rng, least, largest):
    longest = drawn.shape.index(max(drawn.shape))
    spots = []
    for shift in (0, 1):
        where = [jax.random.randint(jax.random.fold_in(rng, axis), (), 0, length) for axis, length in enumerate(drawn.shape)]
        where[longest] = (where[longest] + shift) % drawn.shape[longest]
        spots.append(tuple(where))
    return drawn.at[spots[0]].set(least).at[spots[1]].set(largest)


def levels(own_key, shape, pieces, least, top_value):
    loudness = 1.0
    for dim, shards_of in pieces:
        draws = jax.random.uniform(jax.random.fold_in(jax.random.fold_in(own_key, 6), dim), (shards_of,), jnp.float32, least / len(pieces), top_value / len(pieces))
        loudness = loudness * jnp.repeat(jnp.exp(draws), shape[dim] // shards_of).reshape((-1,) + (1,) * (len(shape) - 1 - dim))
    return loudness


def normal_values(stream_key, extent, spread, bound, cuts=(), kind=jnp.bfloat16):
    loudness = levels(stream_key, extent, cuts, -0.22, 0.18) if cuts else 1.0
    result = jax.random.normal(stream_key, extent, jnp.float32) * spread * loudness
    return jnp.minimum(jnp.maximum(result, -bound), bound).astype(kind)


def setup_inputs(seed: int = 0) -> dict:
    key_of = jax.random.split(jax.random.key(seed), 4)
    records = normal_values(key_of[0], (N_TM, TSUB, CH), 1.0, 6.0, ((0, 4), (1, 8)), jnp.float32)
    chan_order = jax.random.permutation(key_of[1], CH).astype(jnp.int32)
    live_mask = plant((jax.random.randint(key_of[2], (CH,), 0, 10) < 9).astype(jnp.int32), jax.random.fold_in(key_of[2], 1), 0, 1)
    return dict(records=records, chan_order=chan_order, live_mask=live_mask)


def forward_table():
    sample_index = jnp.arange(L, dtype=jnp.int32)
    freq_index = jnp.arange(FB, dtype=jnp.int32)
    phase_step = jnp.mod(sample_index[:, None] * freq_index[None, :], L)
    phase_angle = phase_step.astype(jnp.float32) * (2.0 * math.pi / L)
    return jnp.concatenate([jnp.cos(phase_angle), -jnp.sin(phase_angle)], axis=1)

def smoothing_table():
    freq_index = jnp.arange(FB, dtype=jnp.int32)
    nearby = (jnp.abs(freq_index[:, None] - freq_index[None, :]) <= 2).astype(jnp.float32)
    return nearby / lax.optimization_barrier(jnp.sum(nearby, axis=0, keepdims=True))

def inverse_table():
    freq_index = jnp.arange(FB, dtype=jnp.int32)
    lag_index = jnp.arange(NLAG, dtype=jnp.int32) - NLAG // 2
    phase_step = jnp.mod(freq_index[:, None] * lag_index[None, :], L)
    phase_angle = phase_step.astype(jnp.float32) * (2.0 * math.pi / L)
    edge = (freq_index == 0) | (freq_index == L // 2)
    fold_weight = jnp.where(edge, 1.0, 2.0).astype(jnp.float32) / L
    return jnp.stack([fold_weight[:, None] * jnp.cos(phase_angle), -fold_weight[:, None] * jnp.sin(phase_angle)])

def whiten_spectra(windows, live_block):
    window_mean = lax.optimization_barrier(jnp.mean(windows, axis=-2, keepdims=True))
    centred = windows - window_mean
    normed = centred / jnp.sqrt(lax.optimization_barrier(jnp.mean(centred * centred, axis=-2, keepdims=True)) + 1e-05)
    spectrum = jnp.einsum('...lk,lg->...kg', normed, forward_table(), precision=lax.Precision.HIGHEST)
    real_part = spectrum[..., :FB]
    imag_part = spectrum[..., FB:]
    power = real_part * real_part + imag_part * imag_part
    smoothed = jnp.einsum('...f,fg->...g', power, smoothing_table(), precision=lax.Precision.HIGHEST)
    mean_power = lax.optimization_barrier(jnp.mean(power, axis=-1, keepdims=True))
    scale = live_block.astype(jnp.float32)[:, None] / jnp.sqrt(smoothed + 0.1 * mean_power + 1e-05)
    return jnp.concatenate([real_part * scale, imag_part * scale], axis=-1).astype(jnp.bfloat16)

def reference(records, chan_order, live_mask):
    blocked = jnp.take(records, chan_order, axis=2)
    blocked = blocked.reshape(N_TM, WIN_TM, L, N_CHAN, CH_DEV)
    blocked = jnp.moveaxis(blocked, 3, 0)
    live_blocks = jnp.take(live_mask, chan_order).reshape(N_CHAN, CH_DEV)

    def block_spectra(inputs):
        return whiten_spectra(inputs[0], inputs[1])
    spectra = lax.map(block_spectra, (blocked, live_blocks))
    spectra = spectra.reshape(N_CHAN, N_TM, WIN_TM, CH_DEV, 2, FB)
    inverse = inverse_table()
    results = []
    for round_index in range(ROUNDS):
        offset = max(1, round_index * N_CHAN // 4)

        def one_block(block):
            source = jnp.mod(block - offset, N_CHAN).astype(jnp.int32)
            partner = lax.dynamic_index_in_dim(spectra, source, 0, keepdims=False)
            own_spec = lax.dynamic_index_in_dim(spectra, block, 0, keepdims=False)
            rotated = jnp.concatenate([own_spec[..., 1:2, :], -own_spec[..., 0:1, :]], axis=-2)
            partner = partner.astype(jnp.float32)
            rotated = rotated.astype(jnp.float32)
            own_spec = own_spec.astype(jnp.float32)
            real_sum = jnp.einsum('twicf,twjcf->fji', partner, own_spec, precision=lax.Precision.HIGHEST)
            imag_sum = jnp.einsum('twicf,twjcf->fji', partner, rotated, precision=lax.Precision.HIGHEST)
            return jnp.einsum('cfji,cfl->jil', jnp.stack([real_sum, imag_sum]), inverse, precision=lax.Precision.HIGHEST)
        lagged = lax.map(one_block, jnp.arange(N_CHAN, dtype=jnp.int32))
        results.append(lagged.reshape(N_CHAN * CH_DEV, CH_DEV, NLAG))
    return jnp.stack(results)
```

```python
import math

import jax
import jax.numpy as jnp
from jax import lax
from jax.sharding import PartitionSpec as P

L = 200
FB = 101
NLAG = 128
ROUNDS = 2
WIN_TM = 16


def shifted(block, axis, distance):
    devices = range(lax.axis_size(axis))
    route = [((i - distance) % len(devices), i) for i in devices]
    return lax.ppermute(block, axis, route)


def forward_table():
    sample_index = jnp.arange(L, dtype=jnp.int32)
    freq_index = jnp.arange(FB, dtype=jnp.int32)
    phase_step = jnp.mod(sample_index[:, None] * freq_index[None, :], L)
    phase_angle = phase_step.astype(jnp.float32) * (2.0 * math.pi / L)
    return jnp.concatenate([jnp.cos(phase_angle), -jnp.sin(phase_angle)], axis=1)


def smoothing_table():
    freq_index = jnp.arange(FB, dtype=jnp.int32)
    nearby = (jnp.abs(freq_index[:, None] - freq_index[None, :]) <= 2).astype(jnp.float32)
    return nearby / jnp.sum(nearby, axis=0, keepdims=True)


def inverse_table():
    freq_index = jnp.arange(FB, dtype=jnp.int32)
    lag_index = jnp.arange(NLAG, dtype=jnp.int32) - NLAG // 2
    phase_step = jnp.mod(freq_index[:, None] * lag_index[None, :], L)
    phase_angle = phase_step.astype(jnp.float32) * (2.0 * math.pi / L)
    edge = (freq_index == 0) | (freq_index == L // 2)
    fold_weight = jnp.where(edge, 1.0, 2.0).astype(jnp.float32) / L
    return jnp.stack(
        [fold_weight[:, None] * jnp.cos(phase_angle), -fold_weight[:, None] * jnp.sin(phase_angle)]
    )


def whiten_spectra(windows, live_block, precision=lax.Precision.HIGHEST):
    window_mean = jnp.mean(windows, axis=-2, keepdims=True)
    centred = windows - window_mean
    normed = centred / jnp.sqrt(jnp.mean(centred * centred, axis=-2, keepdims=True) + 1e-05)
    spectrum = jnp.einsum("...lk,lg->...kg", normed, forward_table(), precision=precision)
    real_part = spectrum[..., :FB]
    imag_part = spectrum[..., FB:]
    power = real_part * real_part + imag_part * imag_part
    smoothed = jnp.einsum("...f,fg->...g", power, smoothing_table(), precision=precision)
    mean_power = jnp.mean(power, axis=-1, keepdims=True)
    scale = live_block.astype(jnp.float32)[:, None] / jnp.sqrt(smoothed + 0.1 * mean_power + 1e-05)
    return jnp.concatenate([real_part * scale, imag_part * scale], axis=-1).astype(jnp.bfloat16)


def correlate(partner, own_spec, inverse):
    partner = partner.reshape(partner.shape[0], partner.shape[1], 2, FB)
    own_spec = own_spec.reshape(own_spec.shape[0], own_spec.shape[1], 2, FB)
    rotated = jnp.concatenate([own_spec[:, :, 1:2], -own_spec[:, :, 0:1]], axis=2)
    real_sum = jnp.einsum("wicf,wjcf->fji", partner, own_spec, preferred_element_type=jnp.float32)
    imag_sum = jnp.einsum("wicf,wjcf->fji", partner, rotated, preferred_element_type=jnp.float32)
    return jnp.einsum(
        "cfji,cfl->jil", jnp.stack([real_sum, imag_sum]), inverse, precision=lax.Precision.HIGHEST
    )


def on_device_reduce(records, chan_order, live_mask):
    chan_count = lax.axis_size("chan")
    position = lax.axis_index("chan")
    blocked = jnp.take(records, chan_order, axis=2)
    own_block = lax.all_to_all(blocked, "chan", split_axis=2, concat_axis=1, tiled=True)
    block_width = own_block.shape[2]
    own_windows = own_block.reshape(WIN_TM, L, block_width)
    live_blocks = jnp.take(live_mask, chan_order).reshape(chan_count, block_width)
    own_live = lax.dynamic_index_in_dim(live_blocks, position, 0, keepdims=False)
    own_spectra = whiten_spectra(own_windows, own_live)
    inverse = inverse_table()
    results = []
    for round_index in range(ROUNDS):
        offset = max(1, round_index * chan_count // 4)
        partner_block = shifted(own_windows, "chan", offset)
        source = jnp.mod(position - offset, chan_count)
        partner_live = lax.dynamic_index_in_dim(live_blocks, source, 0, keepdims=False)
        partner = whiten_spectra(partner_block, partner_live)
        lagged = correlate(partner, own_spectra, inverse)
        lagged = lax.psum_scatter(lagged, "tm", scatter_dimension=1, tiled=True)
        results.append(lagged)
    return jnp.stack(results)


def on_device_local(records, chan_order, live_mask):
    chan_count = lax.axis_size("chan")
    tm_count = lax.axis_size("tm")
    tm_position = lax.axis_index("tm")
    samples, channels = records.shape[1], records.shape[2]
    block_width = channels // chan_count
    slice_width = block_width // tm_count
    windows = records.reshape(samples // L, L, channels)
    spectra = whiten_spectra(windows, live_mask, precision=lax.Precision.HIGH)
    spectra = jnp.take(spectra, chan_order, axis=1)
    own = lax.all_to_all(spectra, "chan", split_axis=1, concat_axis=0, tiled=True)
    gathered = lax.all_gather(own, "tm", axis=0, tiled=True)
    windows_all = gathered.shape[0]
    own_spec = gathered.reshape(windows_all, block_width, 2, FB)
    rotated = jnp.concatenate([own_spec[:, :, 1:2], -own_spec[:, :, 0:1]], axis=2)
    both = jnp.concatenate([own_spec, rotated], axis=1)
    my_slice = lax.dynamic_slice_in_dim(gathered, tm_position * slice_width, slice_width, axis=1)
    partners = []
    for round_index in range(ROUNDS):
        offset = max(1, round_index * chan_count // 4)
        partners.append(shifted(my_slice, "chan", offset))
    partner = jnp.concatenate(partners, axis=1).reshape(windows_all, ROUNDS * slice_width, 2, FB)
    sums = jnp.einsum("wicf,wjcf->fji", partner, both, preferred_element_type=jnp.float32)
    sums = sums.reshape(FB, 2, block_width, ROUNDS, slice_width)
    lagged = jnp.einsum(
        "fcjri,cfl->rjil", sums, inverse_table(), precision=lax.Precision.HIGH
    )
    return lagged


def on_device(records, chan_order, live_mask):
    samples = records.shape[1]
    channels = records.shape[2]
    chan_count = lax.axis_size("chan")
    tm_count = lax.axis_size("tm")
    local_ok = (
        samples % L == 0
        and channels % chan_count == 0
        and (channels // chan_count) % tm_count == 0
        and (samples // L) * chan_count == WIN_TM
    )
    if local_ok:
        return on_device_local(records, chan_order, live_mask)
    return on_device_reduce(records, chan_order, live_mask)


def solution(mesh):
    placed = (P("tm", "chan", None), P(), P())
    return jax.shard_map(
        on_device,
        mesh=mesh,
        in_specs=placed,
        out_specs=P(None, "chan", "tm", None),
        check_vma=False,
    )
```

```python
import math

import jax
import jax.numpy as jnp
from jax import lax
from jax.sharding import PartitionSpec as P

L = 200
FB = 101
NLAG = 128
ROUNDS = 2
WIN_TM = 16


def shifted(block, axis, distance):
    devices = range(lax.axis_size(axis))
    route = [((i - distance) % len(devices), i) for i in devices]
    return lax.ppermute(block, axis, route)


def forward_table():
    sample_index = jnp.arange(L, dtype=jnp.int32)
    freq_index = jnp.arange(FB, dtype=jnp.int32)
    phase_step = jnp.mod(sample_index[:, None] * freq_index[None, :], L)
    phase_angle = phase_step.astype(jnp.float32) * (2.0 * math.pi / L)
    return jnp.concatenate([jnp.cos(phase_angle), -jnp.sin(phase_angle)], axis=1)


def smoothing_table():
    freq_index = jnp.arange(FB, dtype=jnp.int32)
    nearby = (jnp.abs(freq_index[:, None] - freq_index[None, :]) <= 2).astype(jnp.float32)
    return nearby / jnp.sum(nearby, axis=0, keepdims=True)


def inverse_table():
    freq_index = jnp.arange(FB, dtype=jnp.int32)
    lag_index = jnp.arange(NLAG, dtype=jnp.int32) - NLAG // 2
    phase_step = jnp.mod(freq_index[:, None] * lag_index[None, :], L)
    phase_angle = phase_step.astype(jnp.float32) * (2.0 * math.pi / L)
    edge = (freq_index == 0) | (freq_index == L // 2)
    fold_weight = jnp.where(edge, 1.0, 2.0).astype(jnp.float32) / L
    return jnp.stack(
        [fold_weight[:, None] * jnp.cos(phase_angle), -fold_weight[:, None] * jnp.sin(phase_angle)]
    )


def whiten_spectra(windows, live_block, precision=lax.Precision.HIGHEST):
    window_mean = jnp.mean(windows, axis=-2, keepdims=True)
    centred = windows - window_mean
    normed = centred / jnp.sqrt(jnp.mean(centred * centred, axis=-2, keepdims=True) + 1e-05)
    spectrum = jnp.einsum("...lk,lg->...kg", normed, forward_table(), precision=precision)
    real_part = spectrum[..., :FB]
    imag_part = spectrum[..., FB:]
    power = real_part * real_part + imag_part * imag_part
    smoothed = jnp.einsum("...f,fg->...g", power, smoothing_table(), precision=precision)
    mean_power = jnp.mean(power, axis=-1, keepdims=True)
    scale = live_block.astype(jnp.float32)[:, None] / jnp.sqrt(smoothed + 0.1 * mean_power + 1e-05)
    return jnp.concatenate([real_part * scale, imag_part * scale], axis=-1).astype(jnp.bfloat16)


def correlate(partner, own_spec, inverse):
    partner = partner.reshape(partner.shape[0], partner.shape[1], 2, FB)
    own_spec = own_spec.reshape(own_spec.shape[0], own_spec.shape[1], 2, FB)
    rotated = jnp.concatenate([own_spec[:, :, 1:2], -own_spec[:, :, 0:1]], axis=2)
    real_sum = jnp.einsum("wicf,wjcf->fji", partner, own_spec, preferred_element_type=jnp.float32)
    imag_sum = jnp.einsum("wicf,wjcf->fji", partner, rotated, preferred_element_type=jnp.float32)
    return jnp.einsum(
        "cfji,cfl->jil", jnp.stack([real_sum, imag_sum]), inverse, precision=lax.Precision.HIGHEST
    )


def on_device_reduce(records, chan_order, live_mask):
    chan_count = lax.axis_size("chan")
    position = lax.axis_index("chan")
    blocked = jnp.take(records, chan_order, axis=2)
    own_block = lax.all_to_all(blocked, "chan", split_axis=2, concat_axis=1, tiled=True)
    block_width = own_block.shape[2]
    own_windows = own_block.reshape(WIN_TM, L, block_width)
    live_blocks = jnp.take(live_mask, chan_order).reshape(chan_count, block_width)
    own_live = lax.dynamic_index_in_dim(live_blocks, position, 0, keepdims=False)
    own_spectra = whiten_spectra(own_windows, own_live)
    inverse = inverse_table()
    results = []
    for round_index in range(ROUNDS):
        offset = max(1, round_index * chan_count // 4)
        partner_block = shifted(own_windows, "chan", offset)
        source = jnp.mod(position - offset, chan_count)
        partner_live = lax.dynamic_index_in_dim(live_blocks, source, 0, keepdims=False)
        partner = whiten_spectra(partner_block, partner_live)
        lagged = correlate(partner, own_spectra, inverse)
        lagged = lax.psum_scatter(lagged, "tm", scatter_dimension=1, tiled=True)
        results.append(lagged)
    return jnp.stack(results)


def whiten_planes(windows, live, precision):
    window_mean = jnp.mean(windows, axis=-2, keepdims=True)
    centred = windows - window_mean
    normed = centred / jnp.sqrt(jnp.mean(centred * centred, axis=-2, keepdims=True) + 1e-05)
    table = forward_table()
    real_part = jnp.einsum("wlk,lg->wkg", normed, table[:, :FB], precision=precision)
    imag_part = jnp.einsum("wlk,lg->wkg", normed, table[:, FB:], precision=precision)
    power = real_part * real_part + imag_part * imag_part
    smoothed = jnp.einsum("wkf,fg->wkg", power, smoothing_table(), precision=precision)
    mean_power = jnp.mean(power, axis=-1, keepdims=True)
    scale = live.astype(jnp.float32)[:, None] / jnp.sqrt(smoothed + 0.1 * mean_power + 1e-05)
    return jnp.stack([real_part * scale, imag_part * scale], axis=1).astype(jnp.bfloat16)


def on_device_local(records, chan_order, live_mask):
    chan_count = lax.axis_size("chan")
    tm_count = lax.axis_size("tm")
    chan_position = lax.axis_index("chan")
    tm_position = lax.axis_index("tm")
    samples, channels = records.shape[1], records.shape[2]
    block_width = channels // chan_count
    slice_width = block_width // tm_count
    windows = records.reshape(samples // L, L, channels)
    spectra = whiten_planes(windows, live_mask, lax.Precision.HIGH)
    sorted_spec = jnp.take(spectra, chan_order, axis=2)
    sorted_spec = sorted_spec.reshape(spectra.shape[0], 2, chan_count, block_width, FB)
    sorted_spec = jnp.moveaxis(sorted_spec, 2, 0)
    pieces = []
    for distance in range(chan_count):
        target = jnp.mod(chan_position + distance, chan_count)
        piece = lax.dynamic_index_in_dim(sorted_spec, target, 0, keepdims=False)
        pieces.append(piece if distance == 0 else shifted(piece, "chan", distance))
    own = jnp.stack(pieces)
    grid = [(c, q) for c in range(chan_count) for q in range(tm_count)]
    partners = []
    for round_index in range(ROUNDS):
        offset = max(1, round_index * chan_count // 4)
        per_source = []
        for tm_shift in range(tm_count):
            target_tm = jnp.mod(tm_position + tm_shift, tm_count)
            piece = lax.dynamic_slice_in_dim(own, target_tm * slice_width, slice_width, axis=3)
            if offset % chan_count == 0 and tm_shift == 0:
                per_source.append(piece)
                continue
            route = [
                (c * tm_count + q, ((c + offset) % chan_count) * tm_count + (q + tm_shift) % tm_count)
                for c, q in grid
            ]
            per_source.append(lax.ppermute(piece, ("chan", "tm"), route))
        by_shift = jnp.stack(per_source)
        by_time = jnp.concatenate([by_shift[::-1], by_shift[::-1]], axis=0)
        start = jnp.mod(tm_count - 1 - tm_position, tm_count)
        by_time = lax.dynamic_slice_in_dim(by_time, start, tm_count, axis=0)
        by_time = jnp.roll(by_time, offset, axis=1)
        partners.append(by_time)
    gathered = lax.all_gather(own, "tm", axis=0, tiled=False)
    windows_all = tm_count * chan_count * spectra.shape[0]
    own_spec = gathered.reshape(windows_all, 2, block_width, FB)
    partner = jnp.concatenate(partners, axis=4).reshape(windows_all, 2, ROUNDS * slice_width, FB)
    rotated = jnp.stack([-partner[:, 1], partner[:, 0]], axis=1)
    both = jnp.concatenate([partner, rotated], axis=2)
    sums = jnp.einsum("xcnf,xcjf->fjn", both, own_spec, preferred_element_type=jnp.float32)
    sums = sums.reshape(FB, block_width, 2, ROUNDS, slice_width)
    lagged = jnp.einsum(
        "fjcri,cfl->rjil", sums, inverse_table(), precision=lax.Precision.HIGH
    )
    return lagged


def on_device(records, chan_order, live_mask):
    samples = records.shape[1]
    channels = records.shape[2]
    chan_count = lax.axis_size("chan")
    tm_count = lax.axis_size("tm")
    local_ok = (
        samples % L == 0
        and channels % chan_count == 0
        and (channels // chan_count) % tm_count == 0
        and (samples // L) * chan_count == WIN_TM
    )
    if local_ok:
        return on_device_local(records, chan_order, live_mask)
    return on_device_reduce(records, chan_order, live_mask)


def solution(mesh):
    placed = (P("tm", "chan", None), P(), P())
    return jax.shard_map(
        on_device,
        mesh=mesh,
        in_specs=placed,
        out_specs=P(None, "chan", "tm", None),
        check_vma=False,
    )
```

```python
import math

import jax
import jax.numpy as jnp
from jax import lax
from jax.sharding import PartitionSpec as P

L = 200
FB = 101
NLAG = 128
ROUNDS = 2
WIN_TM = 16


def shifted(block, axis, distance):
    devices = range(lax.axis_size(axis))
    route = [((i - distance) % len(devices), i) for i in devices]
    return lax.ppermute(block, axis, route)


def forward_table():
    sample_index = jnp.arange(L, dtype=jnp.int32)
    freq_index = jnp.arange(FB, dtype=jnp.int32)
    phase_step = jnp.mod(sample_index[:, None] * freq_index[None, :], L)
    phase_angle = phase_step.astype(jnp.float32) * (2.0 * math.pi / L)
    return jnp.concatenate([jnp.cos(phase_angle), -jnp.sin(phase_angle)], axis=1)


def smoothing_table():
    freq_index = jnp.arange(FB, dtype=jnp.int32)
    nearby = (jnp.abs(freq_index[:, None] - freq_index[None, :]) <= 2).astype(jnp.float32)
    return nearby / jnp.sum(nearby, axis=0, keepdims=True)


def inverse_table():
    freq_index = jnp.arange(FB, dtype=jnp.int32)
    lag_index = jnp.arange(NLAG, dtype=jnp.int32) - NLAG // 2
    phase_step = jnp.mod(freq_index[:, None] * lag_index[None, :], L)
    phase_angle = phase_step.astype(jnp.float32) * (2.0 * math.pi / L)
    edge = (freq_index == 0) | (freq_index == L // 2)
    fold_weight = jnp.where(edge, 1.0, 2.0).astype(jnp.float32) / L
    return jnp.stack(
        [fold_weight[:, None] * jnp.cos(phase_angle), -fold_weight[:, None] * jnp.sin(phase_angle)]
    )


def whiten_spectra(windows, live_block, precision=lax.Precision.HIGHEST):
    window_mean = jnp.mean(windows, axis=-2, keepdims=True)
    centred = windows - window_mean
    normed = centred / jnp.sqrt(jnp.mean(centred * centred, axis=-2, keepdims=True) + 1e-05)
    spectrum = jnp.einsum("...lk,lg->...kg", normed, forward_table(), precision=precision)
    real_part = spectrum[..., :FB]
    imag_part = spectrum[..., FB:]
    power = real_part * real_part + imag_part * imag_part
    smoothed = jnp.einsum("...f,fg->...g", power, smoothing_table(), precision=precision)
    mean_power = jnp.mean(power, axis=-1, keepdims=True)
    scale = live_block.astype(jnp.float32)[:, None] / jnp.sqrt(smoothed + 0.1 * mean_power + 1e-05)
    return jnp.concatenate([real_part * scale, imag_part * scale], axis=-1).astype(jnp.bfloat16)


def correlate(partner, own_spec, inverse):
    partner = partner.reshape(partner.shape[0], partner.shape[1], 2, FB)
    own_spec = own_spec.reshape(own_spec.shape[0], own_spec.shape[1], 2, FB)
    rotated = jnp.concatenate([own_spec[:, :, 1:2], -own_spec[:, :, 0:1]], axis=2)
    real_sum = jnp.einsum("wicf,wjcf->fji", partner, own_spec, preferred_element_type=jnp.float32)
    imag_sum = jnp.einsum("wicf,wjcf->fji", partner, rotated, preferred_element_type=jnp.float32)
    return jnp.einsum(
        "cfji,cfl->jil", jnp.stack([real_sum, imag_sum]), inverse, precision=lax.Precision.HIGHEST
    )


def on_device_reduce(records, chan_order, live_mask):
    chan_count = lax.axis_size("chan")
    position = lax.axis_index("chan")
    blocked = jnp.take(records, chan_order, axis=2)
    own_block = lax.all_to_all(blocked, "chan", split_axis=2, concat_axis=1, tiled=True)
    block_width = own_block.shape[2]
    own_windows = own_block.reshape(WIN_TM, L, block_width)
    live_blocks = jnp.take(live_mask, chan_order).reshape(chan_count, block_width)
    own_live = lax.dynamic_index_in_dim(live_blocks, position, 0, keepdims=False)
    own_spectra = whiten_spectra(own_windows, own_live)
    inverse = inverse_table()
    results = []
    for round_index in range(ROUNDS):
        offset = max(1, round_index * chan_count // 4)
        partner_block = shifted(own_windows, "chan", offset)
        source = jnp.mod(position - offset, chan_count)
        partner_live = lax.dynamic_index_in_dim(live_blocks, source, 0, keepdims=False)
        partner = whiten_spectra(partner_block, partner_live)
        lagged = correlate(partner, own_spectra, inverse)
        lagged = lax.psum_scatter(lagged, "tm", scatter_dimension=1, tiled=True)
        results.append(lagged)
    return jnp.stack(results)


def whiten_planes(windows, live, precision):
    window_mean = jnp.mean(windows, axis=-2, keepdims=True)
    centred = windows - window_mean
    normed = centred / jnp.sqrt(jnp.mean(centred * centred, axis=-2, keepdims=True) + 1e-05)
    table = forward_table()
    real_part = jnp.einsum("wlk,lg->wkg", normed, table[:, :FB], precision=precision)
    imag_part = jnp.einsum("wlk,lg->wkg", normed, table[:, FB:], precision=precision)
    power = real_part * real_part + imag_part * imag_part
    smoothed = jnp.einsum("wkf,fg->wkg", power, smoothing_table(), precision=precision)
    mean_power = jnp.mean(power, axis=-1, keepdims=True)
    scale = live.astype(jnp.float32)[:, None] / jnp.sqrt(smoothed + 0.1 * mean_power + 1e-05)
    return jnp.stack([real_part * scale, imag_part * scale], axis=1).astype(jnp.bfloat16)


def on_device_local(records, chan_order, live_mask):
    chan_count = lax.axis_size("chan")
    tm_count = lax.axis_size("tm")
    chan_position = lax.axis_index("chan")
    tm_position = lax.axis_index("tm")
    samples, channels = records.shape[1], records.shape[2]
    block_width = channels // chan_count
    slice_width = block_width // tm_count
    windows = records.reshape(samples // L, L, channels)
    spectra = whiten_planes(windows, live_mask, lax.Precision.HIGH)
    sorted_spec = jnp.take(spectra, chan_order, axis=2)
    sorted_spec = sorted_spec.reshape(spectra.shape[0], 2, chan_count, block_width, FB)
    sorted_spec = jnp.moveaxis(sorted_spec, 2, 0)
    pieces = []
    for distance in range(chan_count):
        target = jnp.mod(chan_position + distance, chan_count)
        piece = lax.dynamic_index_in_dim(sorted_spec, target, 0, keepdims=False)
        pieces.append(piece if distance == 0 else shifted(piece, "chan", distance))
    own = jnp.stack(pieces)
    grid = [(c, q) for c in range(chan_count) for q in range(tm_count)]
    partners = []
    for round_index in range(ROUNDS):
        offset = max(1, round_index * chan_count // 4)
        per_source = []
        for tm_shift in range(tm_count):
            target_tm = jnp.mod(tm_position + tm_shift, tm_count)
            piece = lax.dynamic_slice_in_dim(own, target_tm * slice_width, slice_width, axis=3)
            if offset % chan_count == 0 and tm_shift == 0:
                per_source.append(piece)
                continue
            route = [
                (c * tm_count + q, ((c + offset) % chan_count) * tm_count + (q + tm_shift) % tm_count)
                for c, q in grid
            ]
            per_source.append(lax.ppermute(piece, ("chan", "tm"), route))
        by_shift = jnp.stack(per_source)
        by_time = jnp.concatenate([by_shift[::-1], by_shift[::-1]], axis=0)
        start = jnp.mod(tm_count - 1 - tm_position, tm_count)
        by_time = lax.dynamic_slice_in_dim(by_time, start, tm_count, axis=0)
        by_time = jnp.roll(by_time, offset, axis=1)
        partners.append(by_time)
    windows_here = chan_count * spectra.shape[0]
    own_t = jnp.transpose(own, (4, 2, 0, 1, 3)).reshape(FB, 2, windows_here, block_width)
    gathered = lax.all_gather(own_t, "tm", axis=2, tiled=False)
    contraction = 2 * tm_count * windows_here
    own_spec = gathered.reshape(FB, contraction, block_width)
    partner = jnp.concatenate(partners, axis=4)
    rotated = jnp.stack([-partner[:, :, :, 1], partner[:, :, :, 0]], axis=3)
    both = jnp.stack([partner, rotated])
    both = jnp.transpose(both, (6, 0, 5, 4, 1, 2, 3))
    both = both.reshape(FB, 2 * ROUNDS * slice_width, contraction)
    sums = jnp.einsum("fnk,fkj->fnj", both, own_spec, preferred_element_type=jnp.float32)
    sums = sums.reshape(FB, 2, ROUNDS, slice_width, block_width)
    lagged = jnp.einsum(
        "fcrij,cfl->rjil", sums, inverse_table(), precision=lax.Precision.HIGH
    )
    return lagged


def on_device(records, chan_order, live_mask):
    samples = records.shape[1]
    channels = records.shape[2]
    chan_count = lax.axis_size("chan")
    tm_count = lax.axis_size("tm")
    local_ok = (
        samples % L == 0
        and channels % chan_count == 0
        and (channels // chan_count) % tm_count == 0
        and (samples // L) * chan_count == WIN_TM
    )
    if local_ok:
        return on_device_local(records, chan_order, live_mask)
    return on_device_reduce(records, chan_order, live_mask)


def solution(mesh):
    placed = (P("tm", "chan", None), P(), P())
    return jax.shard_map(
        on_device,
        mesh=mesh,
        in_specs=placed,
        out_specs=P(None, "chan", "tm", None),
        check_vma=False,
    )
```

```python
import math

import jax
import jax.numpy as jnp
from jax import lax
from jax.sharding import PartitionSpec as P

L = 200
FB = 101
NLAG = 128
ROUNDS = 2
WIN_TM = 16


def shifted(block, axis, distance):
    devices = range(lax.axis_size(axis))
    route = [((i - distance) % len(devices), i) for i in devices]
    return lax.ppermute(block, axis, route)


def forward_table():
    sample_index = jnp.arange(L, dtype=jnp.int32)
    freq_index = jnp.arange(FB, dtype=jnp.int32)
    phase_step = jnp.mod(sample_index[:, None] * freq_index[None, :], L)
    phase_angle = phase_step.astype(jnp.float32) * (2.0 * math.pi / L)
    return jnp.concatenate([jnp.cos(phase_angle), -jnp.sin(phase_angle)], axis=1)


def smoothing_table():
    freq_index = jnp.arange(FB, dtype=jnp.int32)
    nearby = (jnp.abs(freq_index[:, None] - freq_index[None, :]) <= 2).astype(jnp.float32)
    return nearby / jnp.sum(nearby, axis=0, keepdims=True)


def inverse_table():
    freq_index = jnp.arange(FB, dtype=jnp.int32)
    lag_index = jnp.arange(NLAG, dtype=jnp.int32) - NLAG // 2
    phase_step = jnp.mod(freq_index[:, None] * lag_index[None, :], L)
    phase_angle = phase_step.astype(jnp.float32) * (2.0 * math.pi / L)
    edge = (freq_index == 0) | (freq_index == L // 2)
    fold_weight = jnp.where(edge, 1.0, 2.0).astype(jnp.float32) / L
    return jnp.stack(
        [fold_weight[:, None] * jnp.cos(phase_angle), -fold_weight[:, None] * jnp.sin(phase_angle)]
    )


def whiten_spectra(windows, live_block, precision=lax.Precision.HIGHEST):
    window_mean = jnp.mean(windows, axis=-2, keepdims=True)
    centred = windows - window_mean
    normed = centred / jnp.sqrt(jnp.mean(centred * centred, axis=-2, keepdims=True) + 1e-05)
    spectrum = jnp.einsum("...lk,lg->...kg", normed, forward_table(), precision=precision)
    real_part = spectrum[..., :FB]
    imag_part = spectrum[..., FB:]
    power = real_part * real_part + imag_part * imag_part
    smoothed = jnp.einsum("...f,fg->...g", power, smoothing_table(), precision=precision)
    mean_power = jnp.mean(power, axis=-1, keepdims=True)
    scale = live_block.astype(jnp.float32)[:, None] / jnp.sqrt(smoothed + 0.1 * mean_power + 1e-05)
    return jnp.concatenate([real_part * scale, imag_part * scale], axis=-1).astype(jnp.bfloat16)


def correlate(partner, own_spec, inverse):
    partner = partner.reshape(partner.shape[0], partner.shape[1], 2, FB)
    own_spec = own_spec.reshape(own_spec.shape[0], own_spec.shape[1], 2, FB)
    rotated = jnp.concatenate([own_spec[:, :, 1:2], -own_spec[:, :, 0:1]], axis=2)
    real_sum = jnp.einsum("wicf,wjcf->fji", partner, own_spec, preferred_element_type=jnp.float32)
    imag_sum = jnp.einsum("wicf,wjcf->fji", partner, rotated, preferred_element_type=jnp.float32)
    return jnp.einsum(
        "cfji,cfl->jil", jnp.stack([real_sum, imag_sum]), inverse, precision=lax.Precision.HIGHEST
    )


def on_device_reduce(records, chan_order, live_mask):
    chan_count = lax.axis_size("chan")
    position = lax.axis_index("chan")
    blocked = jnp.take(records, chan_order, axis=2)
    own_block = lax.all_to_all(blocked, "chan", split_axis=2, concat_axis=1, tiled=True)
    block_width = own_block.shape[2]
    own_windows = own_block.reshape(WIN_TM, L, block_width)
    live_blocks = jnp.take(live_mask, chan_order).reshape(chan_count, block_width)
    own_live = lax.dynamic_index_in_dim(live_blocks, position, 0, keepdims=False)
    own_spectra = whiten_spectra(own_windows, own_live)
    inverse = inverse_table()
    results = []
    for round_index in range(ROUNDS):
        offset = max(1, round_index * chan_count // 4)
        partner_block = shifted(own_windows, "chan", offset)
        source = jnp.mod(position - offset, chan_count)
        partner_live = lax.dynamic_index_in_dim(live_blocks, source, 0, keepdims=False)
        partner = whiten_spectra(partner_block, partner_live)
        lagged = correlate(partner, own_spectra, inverse)
        lagged = lax.psum_scatter(lagged, "tm", scatter_dimension=1, tiled=True)
        results.append(lagged)
    return jnp.stack(results)


def whiten_planes(windows, live, precision):
    window_mean = jnp.mean(windows, axis=-2, keepdims=True)
    centred = windows - window_mean
    normed = centred / jnp.sqrt(jnp.mean(centred * centred, axis=-2, keepdims=True) + 1e-05)
    table = forward_table()
    real_part = jnp.einsum("wlk,lg->wkg", normed, table[:, :FB], precision=precision)
    imag_part = jnp.einsum("wlk,lg->wkg", normed, table[:, FB:], precision=precision)
    power = real_part * real_part + imag_part * imag_part
    smoothed = jnp.einsum("wkf,fg->wkg", power, smoothing_table(), precision=precision)
    mean_power = jnp.mean(power, axis=-1, keepdims=True)
    scale = live.astype(jnp.float32)[:, None] / jnp.sqrt(smoothed + 0.1 * mean_power + 1e-05)
    return jnp.stack([real_part * scale, imag_part * scale], axis=1).astype(jnp.bfloat16)


def on_device_local(records, chan_order, live_mask):
    chan_count = lax.axis_size("chan")
    tm_count = lax.axis_size("tm")
    chan_position = lax.axis_index("chan")
    tm_position = lax.axis_index("tm")
    samples, channels = records.shape[1], records.shape[2]
    block_width = channels // chan_count
    slice_width = block_width // tm_count
    windows = records.reshape(samples // L, L, channels)
    spectra = whiten_planes(windows, live_mask, lax.Precision.HIGH)
    sorted_spec = jnp.take(spectra, chan_order, axis=2)
    sorted_spec = sorted_spec.reshape(spectra.shape[0], 2, chan_count, block_width, FB)
    sorted_spec = jnp.moveaxis(sorted_spec, 2, 0)
    pieces = []
    for distance in range(chan_count):
        target = jnp.mod(chan_position + distance, chan_count)
        piece = lax.dynamic_index_in_dim(sorted_spec, target, 0, keepdims=False)
        pieces.append(piece if distance == 0 else shifted(piece, "chan", distance))
    own = jnp.stack(pieces)
    masks = [0]
    step = tm_count // 2
    while step >= 1:
        masks = masks + [m ^ step for m in masks]
        step //= 2
    grid = [(c, q) for c in range(chan_count) for q in range(tm_count)]
    partners = []
    for round_index in range(ROUNDS):
        offset = max(1, round_index * chan_count // 4)
        per_source = []
        for mask in masks:
            target_tm = jnp.bitwise_xor(tm_position, mask)
            piece = lax.dynamic_slice_in_dim(own, target_tm * slice_width, slice_width, axis=3)
            route = [
                (c * tm_count + q, ((c + offset) % chan_count) * tm_count + (q ^ mask))
                for c, q in grid
            ]
            per_source.append(lax.ppermute(piece, ("chan", "tm"), route))
        by_time = jnp.stack(per_source)
        by_time = jnp.roll(by_time, offset, axis=1)
        partners.append(by_time)
    windows_here = chan_count * spectra.shape[0]
    own_t = jnp.transpose(own, (4, 2, 0, 1, 3)).reshape(FB, 2, windows_here, block_width)
    gathered = own_t[:, :, None]
    step = tm_count // 2
    while step >= 1:
        route = [(q, q ^ step) for q in range(tm_count)]
        gathered = jnp.concatenate([gathered, lax.ppermute(gathered, "tm", route)], axis=2)
        step //= 2
    contraction = 2 * tm_count * windows_here
    own_spec = gathered.reshape(FB, contraction, block_width)
    partner = jnp.concatenate(partners, axis=4)
    rotated = jnp.stack([-partner[:, :, :, 1], partner[:, :, :, 0]], axis=3)
    both = jnp.stack([partner, rotated])
    both = jnp.transpose(both, (6, 0, 5, 4, 1, 2, 3))
    both = both.reshape(FB, 2 * ROUNDS * slice_width, contraction)
    sums = jnp.einsum("fnk,fkj->fnj", both, own_spec, preferred_element_type=jnp.float32)
    sums = sums.reshape(FB, 2, ROUNDS, slice_width, block_width)
    lagged = jnp.einsum(
        "fcrij,cfl->rjil", sums, inverse_table(), precision=lax.Precision.HIGH
    )
    return lagged


def on_device(records, chan_order, live_mask):
    samples = records.shape[1]
    channels = records.shape[2]
    chan_count = lax.axis_size("chan")
    tm_count = lax.axis_size("tm")
    local_ok = (
        samples % L == 0
        and channels % chan_count == 0
        and (channels // chan_count) % tm_count == 0
        and (samples // L) * chan_count == WIN_TM
    )
    if local_ok:
        return on_device_local(records, chan_order, live_mask)
    return on_device_reduce(records, chan_order, live_mask)


def solution(mesh):
    placed = (P("tm", "chan", None), P(), P())
    return jax.shard_map(
        on_device,
        mesh=mesh,
        in_specs=placed,
        out_specs=P(None, "chan", "tm", None),
        check_vma=False,
    )
```

```python
import math

import jax
import jax.numpy as jnp
from jax import lax
from jax.sharding import PartitionSpec as P

L = 200
FB = 101
NLAG = 128
ROUNDS = 2
WIN_TM = 16


def shifted(block, axis, distance):
    devices = range(lax.axis_size(axis))
    route = [((i - distance) % len(devices), i) for i in devices]
    return lax.ppermute(block, axis, route)


def forward_table():
    sample_index = jnp.arange(L, dtype=jnp.int32)
    freq_index = jnp.arange(FB, dtype=jnp.int32)
    phase_step = jnp.mod(sample_index[:, None] * freq_index[None, :], L)
    phase_angle = phase_step.astype(jnp.float32) * (2.0 * math.pi / L)
    return jnp.concatenate([jnp.cos(phase_angle), -jnp.sin(phase_angle)], axis=1)


def smoothing_table():
    freq_index = jnp.arange(FB, dtype=jnp.int32)
    nearby = (jnp.abs(freq_index[:, None] - freq_index[None, :]) <= 2).astype(jnp.float32)
    return nearby / jnp.sum(nearby, axis=0, keepdims=True)


def inverse_table():
    freq_index = jnp.arange(FB, dtype=jnp.int32)
    lag_index = jnp.arange(NLAG, dtype=jnp.int32) - NLAG // 2
    phase_step = jnp.mod(freq_index[:, None] * lag_index[None, :], L)
    phase_angle = phase_step.astype(jnp.float32) * (2.0 * math.pi / L)
    edge = (freq_index == 0) | (freq_index == L // 2)
    fold_weight = jnp.where(edge, 1.0, 2.0).astype(jnp.float32) / L
    return jnp.stack(
        [fold_weight[:, None] * jnp.cos(phase_angle), -fold_weight[:, None] * jnp.sin(phase_angle)]
    )


def whiten_spectra(windows, live_block, precision=lax.Precision.HIGHEST):
    window_mean = jnp.mean(windows, axis=-2, keepdims=True)
    centred = windows - window_mean
    normed = centred / jnp.sqrt(jnp.mean(centred * centred, axis=-2, keepdims=True) + 1e-05)
    spectrum = jnp.einsum("...lk,lg->...kg", normed, forward_table(), precision=precision)
    real_part = spectrum[..., :FB]
    imag_part = spectrum[..., FB:]
    power = real_part * real_part + imag_part * imag_part
    smoothed = jnp.einsum("...f,fg->...g", power, smoothing_table(), precision=precision)
    mean_power = jnp.mean(power, axis=-1, keepdims=True)
    scale = live_block.astype(jnp.float32)[:, None] / jnp.sqrt(smoothed + 0.1 * mean_power + 1e-05)
    return jnp.concatenate([real_part * scale, imag_part * scale], axis=-1).astype(jnp.bfloat16)


def correlate(partner, own_spec, inverse):
    partner = partner.reshape(partner.shape[0], partner.shape[1], 2, FB)
    own_spec = own_spec.reshape(own_spec.shape[0], own_spec.shape[1], 2, FB)
    rotated = jnp.concatenate([own_spec[:, :, 1:2], -own_spec[:, :, 0:1]], axis=2)
    real_sum = jnp.einsum("wicf,wjcf->fji", partner, own_spec, preferred_element_type=jnp.float32)
    imag_sum = jnp.einsum("wicf,wjcf->fji", partner, rotated, preferred_element_type=jnp.float32)
    return jnp.einsum(
        "cfji,cfl->jil", jnp.stack([real_sum, imag_sum]), inverse, precision=lax.Precision.HIGHEST
    )


def on_device_reduce(records, chan_order, live_mask):
    chan_count = lax.axis_size("chan")
    position = lax.axis_index("chan")
    blocked = jnp.take(records, chan_order, axis=2)
    own_block = lax.all_to_all(blocked, "chan", split_axis=2, concat_axis=1, tiled=True)
    block_width = own_block.shape[2]
    own_windows = own_block.reshape(WIN_TM, L, block_width)
    live_blocks = jnp.take(live_mask, chan_order).reshape(chan_count, block_width)
    own_live = lax.dynamic_index_in_dim(live_blocks, position, 0, keepdims=False)
    own_spectra = whiten_spectra(own_windows, own_live)
    inverse = inverse_table()
    results = []
    for round_index in range(ROUNDS):
        offset = max(1, round_index * chan_count // 4)
        partner_block = shifted(own_windows, "chan", offset)
        source = jnp.mod(position - offset, chan_count)
        partner_live = lax.dynamic_index_in_dim(live_blocks, source, 0, keepdims=False)
        partner = whiten_spectra(partner_block, partner_live)
        lagged = correlate(partner, own_spectra, inverse)
        lagged = lax.psum_scatter(lagged, "tm", scatter_dimension=1, tiled=True)
        results.append(lagged)
    return jnp.stack(results)


def whiten_planes(windows, live, precision):
    window_mean = jnp.mean(windows, axis=-2, keepdims=True)
    centred = windows - window_mean
    normed = centred / jnp.sqrt(jnp.mean(centred * centred, axis=-2, keepdims=True) + 1e-05)
    table = forward_table()
    real_part = jnp.einsum("wlk,lg->wkg", normed, table[:, :FB], precision=precision)
    imag_part = jnp.einsum("wlk,lg->wkg", normed, table[:, FB:], precision=precision)
    power = real_part * real_part + imag_part * imag_part
    smoothed = jnp.einsum("wkf,fg->wkg", power, smoothing_table(), precision=precision)
    mean_power = jnp.mean(power, axis=-1, keepdims=True)
    scale = live.astype(jnp.float32)[:, None] / jnp.sqrt(smoothed + 0.1 * mean_power + 1e-05)
    return jnp.stack([real_part * scale, imag_part * scale], axis=1).astype(jnp.bfloat16)


def on_device_local(records, chan_order, live_mask):
    chan_count = lax.axis_size("chan")
    tm_count = lax.axis_size("tm")
    chan_position = lax.axis_index("chan")
    tm_position = lax.axis_index("tm")
    samples, channels = records.shape[1], records.shape[2]
    block_width = channels // chan_count
    slice_width = block_width // tm_count
    windows = records.reshape(samples // L, L, channels)
    spectra = whiten_planes(windows, live_mask, lax.Precision.HIGH)
    sorted_spec = jnp.take(spectra, chan_order, axis=2)
    sorted_spec = sorted_spec.reshape(spectra.shape[0], 2, chan_count, block_width, FB)
    sorted_spec = jnp.moveaxis(sorted_spec, 2, 0)
    offsets = [max(1, round_index * chan_count // 4) for round_index in range(ROUNDS)]
    pieces = []
    for distance in range(chan_count):
        wanted = [chan_position + distance] + [chan_position + distance - o for o in offsets]
        piece = jnp.stack(
            [lax.dynamic_index_in_dim(sorted_spec, jnp.mod(b, chan_count), 0, keepdims=False) for b in wanted]
        )
        pieces.append(piece if distance == 0 else shifted(piece, "chan", distance))
    exchanged = jnp.stack(pieces)
    own = exchanged[:, 0]
    windows_here = chan_count * spectra.shape[0]
    own_t = jnp.transpose(own, (4, 2, 0, 1, 3)).reshape(FB, 2, windows_here, block_width)
    targets = list(range(tm_count))
    held = []
    for round_index in range(ROUNDS):
        block = exchanged[:, 1 + round_index]
        held.append(jnp.stack([
            lax.dynamic_slice_in_dim(block, jnp.bitwise_xor(tm_position, r) * slice_width, slice_width, axis=3)
            for r in targets
        ])[None])
    gathered = own_t[:, :, None]
    step = tm_count // 2
    while step >= 1:
        send_at = [n for n, r in enumerate(targets) if r & step]
        keep_at = [n for n, r in enumerate(targets) if not r & step]
        route = [(q, q ^ step) for q in range(tm_count)]
        payload = (gathered, [h[:, send_at[0]:send_at[-1] + 1] for h in held])
        got_own, got_held = lax.ppermute(payload, "tm", route)
        gathered = jnp.concatenate([gathered, got_own], axis=2)
        held = [
            jnp.concatenate([h[:, keep_at[0]:keep_at[-1] + 1], g], axis=0)
            for h, g in zip(held, got_held)
        ]
        targets = [targets[n] for n in keep_at]
        step //= 2
    partners = [h[:, 0] for h in held]
    contraction = 2 * tm_count * windows_here
    own_spec = gathered.reshape(FB, contraction, block_width)
    partner = jnp.concatenate(partners, axis=4)
    rotated = jnp.stack([-partner[:, :, :, 1], partner[:, :, :, 0]], axis=3)
    both = jnp.stack([partner, rotated])
    both = jnp.transpose(both, (6, 0, 5, 4, 1, 2, 3))
    both = both.reshape(FB, 2 * ROUNDS * slice_width, contraction)
    sums = jnp.einsum("fnk,fkj->fnj", both, own_spec, preferred_element_type=jnp.float32)
    sums = sums.reshape(FB, 2, ROUNDS, slice_width, block_width)
    lagged = jnp.einsum(
        "fcrij,cfl->rjil", sums, inverse_table(), precision=lax.Precision.HIGH
    )
    return lagged


def on_device(records, chan_order, live_mask):
    samples = records.shape[1]
    channels = records.shape[2]
    chan_count = lax.axis_size("chan")
    tm_count = lax.axis_size("tm")
    local_ok = (
        samples % L == 0
        and channels % chan_count == 0
        and (channels // chan_count) % tm_count == 0
        and (samples // L) * chan_count == WIN_TM
    )
    if local_ok:
        return on_device_local(records, chan_order, live_mask)
    return on_device_reduce(records, chan_order, live_mask)


def solution(mesh):
    placed = (P("tm", "chan", None), P(), P())
    return jax.shard_map(
        on_device,
        mesh=mesh,
        in_specs=placed,
        out_specs=P(None, "chan", "tm", None),
        check_vma=False,
    )
```

```python
import math

import jax
import jax.numpy as jnp
from jax import lax
from jax.sharding import PartitionSpec as P

L = 200
FB = 101
NLAG = 128
ROUNDS = 2
WIN_TM = 16


def shifted(block, axis, distance):
    devices = range(lax.axis_size(axis))
    route = [((i - distance) % len(devices), i) for i in devices]
    return lax.ppermute(block, axis, route)


def forward_table():
    sample_index = jnp.arange(L, dtype=jnp.int32)
    freq_index = jnp.arange(FB, dtype=jnp.int32)
    phase_step = jnp.mod(sample_index[:, None] * freq_index[None, :], L)
    phase_angle = phase_step.astype(jnp.float32) * (2.0 * math.pi / L)
    return jnp.concatenate([jnp.cos(phase_angle), -jnp.sin(phase_angle)], axis=1)


def smoothing_table():
    freq_index = jnp.arange(FB, dtype=jnp.int32)
    nearby = (jnp.abs(freq_index[:, None] - freq_index[None, :]) <= 2).astype(jnp.float32)
    return nearby / jnp.sum(nearby, axis=0, keepdims=True)


def inverse_table():
    freq_index = jnp.arange(FB, dtype=jnp.int32)
    lag_index = jnp.arange(NLAG, dtype=jnp.int32) - NLAG // 2
    phase_step = jnp.mod(freq_index[:, None] * lag_index[None, :], L)
    phase_angle = phase_step.astype(jnp.float32) * (2.0 * math.pi / L)
    edge = (freq_index == 0) | (freq_index == L // 2)
    fold_weight = jnp.where(edge, 1.0, 2.0).astype(jnp.float32) / L
    return jnp.stack(
        [fold_weight[:, None] * jnp.cos(phase_angle), -fold_weight[:, None] * jnp.sin(phase_angle)]
    )


def whiten_spectra(windows, live_block, precision=lax.Precision.HIGHEST):
    window_mean = jnp.mean(windows, axis=-2, keepdims=True)
    centred = windows - window_mean
    normed = centred / jnp.sqrt(jnp.mean(centred * centred, axis=-2, keepdims=True) + 1e-05)
    spectrum = jnp.einsum("...lk,lg->...kg", normed, forward_table(), precision=precision)
    real_part = spectrum[..., :FB]
    imag_part = spectrum[..., FB:]
    power = real_part * real_part + imag_part * imag_part
    smoothed = jnp.einsum("...f,fg->...g", power, smoothing_table(), precision=precision)
    mean_power = jnp.mean(power, axis=-1, keepdims=True)
    scale = live_block.astype(jnp.float32)[:, None] / jnp.sqrt(smoothed + 0.1 * mean_power + 1e-05)
    return jnp.concatenate([real_part * scale, imag_part * scale], axis=-1).astype(jnp.bfloat16)


def correlate(partner, own_spec, inverse):
    partner = partner.reshape(partner.shape[0], partner.shape[1], 2, FB)
    own_spec = own_spec.reshape(own_spec.shape[0], own_spec.shape[1], 2, FB)
    rotated = jnp.concatenate([own_spec[:, :, 1:2], -own_spec[:, :, 0:1]], axis=2)
    real_sum = jnp.einsum("wicf,wjcf->fji", partner, own_spec, preferred_element_type=jnp.float32)
    imag_sum = jnp.einsum("wicf,wjcf->fji", partner, rotated, preferred_element_type=jnp.float32)
    return jnp.einsum(
        "cfji,cfl->jil", jnp.stack([real_sum, imag_sum]), inverse, precision=lax.Precision.HIGHEST
    )


def on_device_reduce(records, chan_order, live_mask):
    chan_count = lax.axis_size("chan")
    position = lax.axis_index("chan")
    blocked = jnp.take(records, chan_order, axis=2)
    own_block = lax.all_to_all(blocked, "chan", split_axis=2, concat_axis=1, tiled=True)
    block_width = own_block.shape[2]
    own_windows = own_block.reshape(WIN_TM, L, block_width)
    live_blocks = jnp.take(live_mask, chan_order).reshape(chan_count, block_width)
    own_live = lax.dynamic_index_in_dim(live_blocks, position, 0, keepdims=False)
    own_spectra = whiten_spectra(own_windows, own_live)
    inverse = inverse_table()
    results = []
    for round_index in range(ROUNDS):
        offset = max(1, round_index * chan_count // 4)
        partner_block = shifted(own_windows, "chan", offset)
        source = jnp.mod(position - offset, chan_count)
        partner_live = lax.dynamic_index_in_dim(live_blocks, source, 0, keepdims=False)
        partner = whiten_spectra(partner_block, partner_live)
        lagged = correlate(partner, own_spectra, inverse)
        lagged = lax.psum_scatter(lagged, "tm", scatter_dimension=1, tiled=True)
        results.append(lagged)
    return jnp.stack(results)


def whiten_planes(windows, live, precision):
    window_mean = jnp.mean(windows, axis=-2, keepdims=True)
    centred = windows - window_mean
    normed = centred / jnp.sqrt(jnp.mean(centred * centred, axis=-2, keepdims=True) + 1e-05)
    table = forward_table()
    real_part = jnp.einsum("wlk,lg->wkg", normed, table[:, :FB], precision=precision)
    imag_part = jnp.einsum("wlk,lg->wkg", normed, table[:, FB:], precision=precision)
    power = real_part * real_part + imag_part * imag_part
    smoothed = jnp.einsum("wkf,fg->wkg", power, smoothing_table(), precision=precision)
    mean_power = jnp.mean(power, axis=-1, keepdims=True)
    scale = live.astype(jnp.float32)[:, None] / jnp.sqrt(smoothed + 0.1 * mean_power + 1e-05)
    return jnp.stack([real_part * scale, imag_part * scale], axis=1).astype(jnp.bfloat16)


def on_device_local(records, chan_order, live_mask):
    chan_count = lax.axis_size("chan")
    tm_count = lax.axis_size("tm")
    chan_position = lax.axis_index("chan")
    tm_position = lax.axis_index("tm")
    samples, channels = records.shape[1], records.shape[2]
    block_width = channels // chan_count
    slice_width = block_width // tm_count
    windows = records.reshape(samples // L, L, channels)
    spectra = whiten_planes(windows, live_mask, lax.Precision.HIGH)
    sorted_spec = jnp.take(spectra, chan_order, axis=2)
    sorted_spec = sorted_spec.reshape(spectra.shape[0], 2, chan_count, block_width, FB)
    sorted_spec = jnp.moveaxis(sorted_spec, 2, 0)
    pieces = []
    for distance in range(chan_count):
        target = jnp.mod(chan_position + distance, chan_count)
        piece = lax.dynamic_index_in_dim(sorted_spec, target, 0, keepdims=False)
        pieces.append(piece if distance == 0 else shifted(piece, "chan", distance))
    own = jnp.stack(pieces)
    gathered = own[None]
    step = tm_count // 2
    while step >= 1:
        route = [(q, q ^ step) for q in range(tm_count)]
        gathered = jnp.concatenate([gathered, lax.ppermute(gathered, "tm", route)], axis=0)
        step //= 2
    windows_all = gathered.shape[0] * gathered.shape[1] * gathered.shape[2]
    own_spec = jnp.transpose(gathered, (5, 3, 0, 1, 2, 4)).reshape(FB, 2 * windows_all, block_width)
    my_slice = lax.dynamic_slice_in_dim(gathered, tm_position * slice_width, slice_width, axis=4)
    inverse = inverse_table()
    results = []
    for round_index in range(ROUNDS):
        offset = max(1, round_index * chan_count // 4)
        partner = shifted(my_slice, "chan", offset)
        partner = jnp.roll(partner, offset, axis=1)
        rotated = jnp.stack([-partner[:, :, :, 1], partner[:, :, :, 0]], axis=3)
        both = jnp.stack([partner, rotated])
        both = jnp.transpose(both, (6, 0, 5, 4, 1, 2, 3)).reshape(FB, 2 * slice_width, 2 * windows_all)
        sums = jnp.einsum("fnk,fkj->fnj", both, own_spec, preferred_element_type=jnp.float32)
        sums = sums.reshape(FB, 2, slice_width, block_width)
        results.append(
            jnp.einsum("fcij,cfl->jil", sums, inverse, precision=lax.Precision.HIGH)
        )
    return jnp.stack(results)


def on_device(records, chan_order, live_mask):
    samples = records.shape[1]
    channels = records.shape[2]
    chan_count = lax.axis_size("chan")
    tm_count = lax.axis_size("tm")
    local_ok = (
        samples % L == 0
        and channels % chan_count == 0
        and (channels // chan_count) % tm_count == 0
        and (samples // L) * chan_count == WIN_TM
    )
    if local_ok:
        return on_device_local(records, chan_order, live_mask)
    return on_device_reduce(records, chan_order, live_mask)


def solution(mesh):
    placed = (P("tm", "chan", None), P(), P())
    return jax.shard_map(
        on_device,
        mesh=mesh,
        in_specs=placed,
        out_specs=P(None, "chan", "tm", None),
        check_vma=False,
    )
```

```python
import math

import jax
import jax.numpy as jnp
from jax import lax
from jax.sharding import PartitionSpec as P

L = 200
FB = 101
NLAG = 128
ROUNDS = 2
WIN_TM = 16


def shifted(block, axis, distance):
    devices = range(lax.axis_size(axis))
    route = [((i - distance) % len(devices), i) for i in devices]
    return lax.ppermute(block, axis, route)


def forward_table():
    sample_index = jnp.arange(L, dtype=jnp.int32)
    freq_index = jnp.arange(FB, dtype=jnp.int32)
    phase_step = jnp.mod(sample_index[:, None] * freq_index[None, :], L)
    phase_angle = phase_step.astype(jnp.float32) * (2.0 * math.pi / L)
    return jnp.concatenate([jnp.cos(phase_angle), -jnp.sin(phase_angle)], axis=1)


def smoothing_table():
    freq_index = jnp.arange(FB, dtype=jnp.int32)
    nearby = (jnp.abs(freq_index[:, None] - freq_index[None, :]) <= 2).astype(jnp.float32)
    return nearby / jnp.sum(nearby, axis=0, keepdims=True)


def inverse_table():
    freq_index = jnp.arange(FB, dtype=jnp.int32)
    lag_index = jnp.arange(NLAG, dtype=jnp.int32) - NLAG // 2
    phase_step = jnp.mod(freq_index[:, None] * lag_index[None, :], L)
    phase_angle = phase_step.astype(jnp.float32) * (2.0 * math.pi / L)
    edge = (freq_index == 0) | (freq_index == L // 2)
    fold_weight = jnp.where(edge, 1.0, 2.0).astype(jnp.float32) / L
    return jnp.stack(
        [fold_weight[:, None] * jnp.cos(phase_angle), -fold_weight[:, None] * jnp.sin(phase_angle)]
    )


def whiten_spectra(windows, live_block, precision=lax.Precision.HIGHEST):
    window_mean = jnp.mean(windows, axis=-2, keepdims=True)
    centred = windows - window_mean
    normed = centred / jnp.sqrt(jnp.mean(centred * centred, axis=-2, keepdims=True) + 1e-05)
    spectrum = jnp.einsum("...lk,lg->...kg", normed, forward_table(), precision=precision)
    real_part = spectrum[..., :FB]
    imag_part = spectrum[..., FB:]
    power = real_part * real_part + imag_part * imag_part
    smoothed = jnp.einsum("...f,fg->...g", power, smoothing_table(), precision=precision)
    mean_power = jnp.mean(power, axis=-1, keepdims=True)
    scale = live_block.astype(jnp.float32)[:, None] / jnp.sqrt(smoothed + 0.1 * mean_power + 1e-05)
    return jnp.concatenate([real_part * scale, imag_part * scale], axis=-1).astype(jnp.bfloat16)


def correlate(partner, own_spec, inverse):
    partner = partner.reshape(partner.shape[0], partner.shape[1], 2, FB)
    own_spec = own_spec.reshape(own_spec.shape[0], own_spec.shape[1], 2, FB)
    rotated = jnp.concatenate([own_spec[:, :, 1:2], -own_spec[:, :, 0:1]], axis=2)
    real_sum = jnp.einsum("wicf,wjcf->fji", partner, own_spec, preferred_element_type=jnp.float32)
    imag_sum = jnp.einsum("wicf,wjcf->fji", partner, rotated, preferred_element_type=jnp.float32)
    return jnp.einsum(
        "cfji,cfl->jil", jnp.stack([real_sum, imag_sum]), inverse, precision=lax.Precision.HIGHEST
    )


def on_device_reduce(records, chan_order, live_mask):
    chan_count = lax.axis_size("chan")
    position = lax.axis_index("chan")
    blocked = jnp.take(records, chan_order, axis=2)
    own_block = lax.all_to_all(blocked, "chan", split_axis=2, concat_axis=1, tiled=True)
    block_width = own_block.shape[2]
    own_windows = own_block.reshape(WIN_TM, L, block_width)
    live_blocks = jnp.take(live_mask, chan_order).reshape(chan_count, block_width)
    own_live = lax.dynamic_index_in_dim(live_blocks, position, 0, keepdims=False)
    own_spectra = whiten_spectra(own_windows, own_live)
    inverse = inverse_table()
    results = []
    for round_index in range(ROUNDS):
        offset = max(1, round_index * chan_count // 4)
        partner_block = shifted(own_windows, "chan", offset)
        source = jnp.mod(position - offset, chan_count)
        partner_live = lax.dynamic_index_in_dim(live_blocks, source, 0, keepdims=False)
        partner = whiten_spectra(partner_block, partner_live)
        lagged = correlate(partner, own_spectra, inverse)
        lagged = lax.psum_scatter(lagged, "tm", scatter_dimension=1, tiled=True)
        results.append(lagged)
    return jnp.stack(results)


def whiten_planes(windows, live, precision):
    window_mean = jnp.mean(windows, axis=-2, keepdims=True)
    centred = windows - window_mean
    normed = centred / jnp.sqrt(jnp.mean(centred * centred, axis=-2, keepdims=True) + 1e-05)
    table = forward_table()
    real_part = jnp.einsum("wlk,lg->wkg", normed, table[:, :FB], precision=precision)
    imag_part = jnp.einsum("wlk,lg->wkg", normed, table[:, FB:], precision=precision)
    power = real_part * real_part + imag_part * imag_part
    smoothed = jnp.einsum("wkf,fg->wkg", power, smoothing_table(), precision=precision)
    mean_power = jnp.mean(power, axis=-1, keepdims=True)
    scale = live.astype(jnp.float32)[:, None] / jnp.sqrt(smoothed + 0.1 * mean_power + 1e-05)
    return jnp.stack([real_part * scale, imag_part * scale], axis=1).astype(jnp.bfloat16)


def on_device_local(records, chan_order, live_mask):
    chan_count = lax.axis_size("chan")
    tm_count = lax.axis_size("tm")
    chan_position = lax.axis_index("chan")
    tm_position = lax.axis_index("tm")
    samples, channels = records.shape[1], records.shape[2]
    block_width = channels // chan_count
    slice_width = block_width // tm_count
    windows = records.reshape(samples // L, L, channels)
    spectra = whiten_planes(windows, live_mask, lax.Precision.HIGH)
    sorted_spec = jnp.take(spectra, chan_order, axis=2)
    sorted_spec = sorted_spec.reshape(spectra.shape[0], 2, chan_count, block_width, FB)
    sorted_spec = jnp.moveaxis(sorted_spec, 2, 0)
    pieces = []
    for distance in range(chan_count):
        target = jnp.mod(chan_position + distance, chan_count)
        piece = lax.dynamic_index_in_dim(sorted_spec, target, 0, keepdims=False)
        pieces.append(piece if distance == 0 else shifted(piece, "chan", distance))
    own = jnp.stack(pieces)
    offsets = [max(1, round_index * chan_count // 4) for round_index in range(ROUNDS)]

    def send_slices(group):
        piece = lax.dynamic_slice_in_dim(group, tm_position * slice_width, slice_width, axis=4)
        return [shifted(piece, "chan", offset) for offset in offsets]

    gathered = own[None]
    partner_groups = [send_slices(gathered)]
    step = tm_count // 2
    while step >= 1:
        route = [(q, q ^ step) for q in range(tm_count)]
        arrived = lax.ppermute(gathered, "tm", route)
        partner_groups.append(send_slices(arrived))
        gathered = jnp.concatenate([gathered, arrived], axis=0)
        step //= 2
    windows_all = gathered.shape[0] * gathered.shape[1] * gathered.shape[2]
    own_spec = jnp.transpose(gathered, (5, 3, 0, 1, 2, 4)).reshape(FB, 2 * windows_all, block_width)
    inverse = inverse_table()
    results = []
    for round_index in range(ROUNDS):
        offset = max(1, round_index * chan_count // 4)
        partner_block = shifted(own_windows, "chan", offset)
        source = jnp.mod(position - offset, chan_count)
        partner_live = lax.dynamic_index_in_dim(live_blocks, source, 0, keepdims=False)
        partner = whiten_spectra(partner_block, partner_live)
        lagged = correlate(partner, own_spectra, inverse)
        lagged = lax.psum_scatter(lagged, "tm", scatter_dimension=1, tiled=True)
        results.append(lagged)
    return jnp.stack(results)


def whiten_planes(windows, live, precision):
    window_mean = jnp.mean(windows, axis=-2, keepdims=True)
    centred = windows - window_mean
    normed = centred / jnp.sqrt(jnp.mean(centred * centred, axis=-2, keepdims=True) + 1e-05)
    table = forward_table()
    real_part = jnp.einsum("wlk,lg->wkg", normed, table[:, :FB], precision=precision)
    imag_part = jnp.einsum("wlk,lg->wkg", normed, table[:, FB:], precision=precision)
    power = real_part * real_part + imag_part * imag_part
    smoothed = jnp.einsum("wkf,fg->wkg", power, smoothing_table(), precision=precision)
    mean_power = jnp.mean(power, axis=-1, keepdims=True)
    scale = live.astype(jnp.float32)[:, None] / jnp.sqrt(smoothed + 0.1 * mean_power + 1e-05)
    return jnp.stack([real_part * scale, imag_part * scale], axis=1).astype(jnp.bfloat16)


def on_device_local(records, chan_order, live_mask):
    chan_count = lax.axis_size("chan")
    tm_count = lax.axis_size("tm")
    chan_position = lax.axis_index("chan")
    tm_position = lax.axis_index("tm")
    samples, channels = records.shape[1], records.shape[2]
    block_width = channels // chan_count
    slice_width = block_width // tm_count
    windows = records.reshape(samples // L, L, channels)
    spectra = whiten_planes(windows, live_mask, lax.Precision.HIGH)
    sorted_spec = jnp.take(spectra, chan_order, axis=2)
    sorted_spec = sorted_spec.reshape(spectra.shape[0], 2, chan_count, block_width, FB)
    sorted_spec = jnp.moveaxis(sorted_spec, 2, 0)
    pieces = []
    for distance in range(chan_count):
        target = jnp.mod(chan_position + distance, chan_count)
        piece = lax.dynamic_index_in_dim(sorted_spec, target, 0, keepdims=False)
        pieces.append(piece if distance == 0 else shifted(piece, "chan", distance))
    own = jnp.stack(pieces)
    offsets = [max(1, round_index * chan_count // 4) for round_index in range(ROUNDS)]

    def send_slices(group):
        piece = lax.dynamic_slice_in_dim(group, tm_position * slice_width, slice_width, axis=4)
        return [shifted(piece, "chan", offset) for offset in offsets]

    gathered = own[None]
    partner_groups = [send_slices(gathered)]
    step = tm_count // 2
    while step >= 1:
        route = [(q, q ^ step) for q in range(tm_count)]
        arrived = lax.ppermute(gathered, "tm", route)
        partner_groups.append(send_slices(arrived))
        gathered = jnp.concatenate([gathered, arrived], axis=0)
        step //= 2
    windows_all = gathered.shape[0] * gathered.shape[1] * gathered.shape[2]
    own_spec = jnp.transpose(gathered, (5, 3, 0, 1, 2, 4)).reshape(FB, 2 * windows_all, block_width)
    inverse = inverse_table()
    results = []
    for round_index in range(ROUNDS):
        offset = offsets[round_index]
        partner = jnp.concatenate([group[round_index] for group in partner_groups], axis=0)
        partner = jnp.roll(partner, offset, axis=1)
        rotated = jnp.stack([-partner[:, :, :, 1], partner[:, :, :, 0]], axis=3)
        both = jnp.stack([partner, rotated])
        both = jnp.transpose(both, (6, 0, 5, 4, 1, 2, 3)).reshape(FB, 2 * slice_width, 2 * windows_all)
        sums = jnp.einsum("fnk,fkj->fnj", both, own_spec, preferred_element_type=jnp.float32)
        sums = sums.reshape(FB, 2, slice_width, block_width)
        results.append(
            jnp.einsum("fcij,cfl->jil", sums, inverse, precision=lax.Precision.HIGH)
        )
    return jnp.stack(results)


def on_device(records, chan_order, live_mask):
    samples = records.shape[1]
    channels = records.shape[2]
    chan_count = lax.axis_size("chan")
    tm_count = lax.axis_size("tm")
    local_ok = (
        samples % L == 0
        and channels % chan_count == 0
        and (channels // chan_count) % tm_count == 0
        and (samples // L) * chan_count == WIN_TM
    )
    if local_ok:
        return on_device_local(records, chan_order, live_mask)
    return on_device_reduce(records, chan_order, live_mask)


def solution(mesh):
    placed = (P("tm", "chan", None), P(), P())
    return jax.shard_map(
        on_device,
        mesh=mesh,
        in_specs=placed,
        out_specs=P(None, "chan", "tm", None),
        check_vma=False,
    )
```

```python
import math

import jax
import jax.numpy as jnp
from jax import lax
from jax.sharding import PartitionSpec as P


L = 200
FB = 101
NLAG = 128
ROUNDS = 2
WIN_TM = 16


def shifted(block, axis, distance):
    devices = range(lax.axis_size(axis))
    route = [((i - distance) % len(devices), i) for i in devices]
    return lax.ppermute(block, axis, route)


def forward_table():
    sample_index = jnp.arange(L, dtype=jnp.int32)
    freq_index = jnp.arange(FB, dtype=jnp.int32)
    phase_step = jnp.mod(sample_index[:, None] * freq_index[None, :], L)
    phase_angle = phase_step.astype(jnp.float32) * (2.0 * math.pi / L)
    return jnp.concatenate([jnp.cos(phase_angle), -jnp.sin(phase_angle)], axis=1)


def smoothing_table():
    freq_index = jnp.arange(FB, dtype=jnp.int32)
    nearby = (jnp.abs(freq_index[:, None] - freq_index[None, :]) <= 2).astype(jnp.float32)
    return nearby / jnp.sum(nearby, axis=0, keepdims=True)


def inverse_table():
    freq_index = jnp.arange(FB, dtype=jnp.int32)
    lag_index = jnp.arange(NLAG, dtype=jnp.int32) - NLAG // 2
    phase_step = jnp.mod(freq_index[:, None] * lag_index[None, :], L)
    phase_angle = phase_step.astype(jnp.float32) * (2.0 * math.pi / L)
    edge = (freq_index == 0) | (freq_index == L // 2)
    fold_weight = jnp.where(edge, 1.0, 2.0).astype(jnp.float32) / L
    return jnp.stack(
        [fold_weight[:, None] * jnp.cos(phase_angle), -fold_weight[:, None] * jnp.sin(phase_angle)]
    )


def whiten_spectra(windows, live_block, precision=lax.Precision.HIGHEST):
    window_mean = jnp.mean(windows, axis=-2, keepdims=True)
    centred = windows - window_mean
    normed = centred / jnp.sqrt(jnp.mean(centred * centred, axis=-2, keepdims=True) + 1e-05)
    spectrum = jnp.einsum("...lk,lg->...kg", normed, forward_table(), precision=precision)
    real_part = spectrum[..., :FB]
    imag_part = spectrum[..., FB:]
    power = real_part * real_part + imag_part * imag_part
    smoothed = jnp.einsum("...f,fg->...g", power, smoothing_table(), precision=precision)
    mean_power = jnp.mean(power, axis=-1, keepdims=True)
    scale = live_block.astype(jnp.float32)[:, None] / jnp.sqrt(smoothed + 0.1 * mean_power + 1e-05)
    return jnp.concatenate([real_part * scale, imag_part * scale], axis=-1).astype(jnp.bfloat16)


def correlate(partner, own_spec, inverse):
    partner = partner.reshape(partner.shape[0], partner.shape[1], 2, FB)
    own_spec = own_spec.reshape(own_spec.shape[0], own_spec.shape[1], 2, FB)
    rotated = jnp.concatenate([own_spec[:, :, 1:2], -own_spec[:, :, 0:1]], axis=2)
    real_sum = jnp.einsum("wicf,wjcf->fji", partner, own_spec, preferred_element_type=jnp.float32)
    imag_sum = jnp.einsum("wicf,wjcf->fji", partner, rotated, preferred_element_type=jnp.float32)
    return jnp.einsum(
        "cfji,cfl->jil", jnp.stack([real_sum, imag_sum]), inverse, precision=lax.Precision.HIGHEST
    )


def on_device_reduce(records, chan_order, live_mask):
    chan_count = lax.axis_size("chan")
    position = lax.axis_index("chan")
    blocked = jnp.take(records, chan_order, axis=2)
    own_block = lax.all_to_all(blocked, "chan", split_axis=2, concat_axis=1, tiled=True)
    block_width = own_block.shape[2]
    own_windows = own_block.reshape(WIN_TM, L, block_width)
    live_blocks = jnp.take(live_mask, chan_order).reshape(chan_count, block_width)
    own_live = lax.dynamic_index_in_dim(live_blocks, position, 0, keepdims=False)
    own_spectra = whiten_spectra(own_windows, own_live)
    inverse = inverse_table()
    results = []
    for round_index in range(ROUNDS):
        offset = max(1, round_index * chan_count // 4)
        partner_block = shifted(own_windows, "chan", offset)
        source = jnp.mod(position - offset, chan_count)
        partner_live = lax.dynamic_index_in_dim(live_blocks, source, 0, keepdims=False)
        partner = whiten_spectra(partner_block, partner_live)
        lagged = correlate(partner, own_spectra, inverse)
        lagged = lax.psum_scatter(lagged, "tm", scatter_dimension=1, tiled=True)
        results.append(lagged)
    return jnp.stack(results)


def whiten_planes(windows, live, precision):
    window_mean = jnp.mean(windows, axis=-2, keepdims=True)
    centred = windows - window_mean
    normed = centred / jnp.sqrt(jnp.mean(centred * centred, axis=-2, keepdims=True) + 1e-05)
    table = forward_table()
    real_part = jnp.einsum("wlk,lg->wkg", normed, table[:, :FB], precision=precision)
    imag_part = jnp.einsum("wlk,lg->wkg", normed, table[:, FB:], precision=precision)
    power = real_part * real_part + imag_part * imag_part
    smoothed = jnp.einsum("wkf,fg->wkg", power, smoothing_table(), precision=precision)
    mean_power = jnp.mean(power, axis=-1, keepdims=True)
    scale = live.astype(jnp.float32)[:, None] / jnp.sqrt(smoothed + 0.1 * mean_power + 1e-05)
    return jnp.stack([real_part * scale, imag_part * scale], axis=1).astype(jnp.bfloat16)


def on_device_local(records, chan_order, live_mask):
    chan_count = lax.axis_size("chan")
    tm_count = lax.axis_size("tm")
    chan_position = lax.axis_index("chan")
    tm_position = lax.axis_index("tm")
    samples, channels = records.shape[1], records.shape[2]
    block_width = channels // chan_count
    slice_width = block_width // tm_count
    windows = records.reshape(samples // L, L, channels)
    spectra = whiten_planes(windows, live_mask, lax.Precision.HIGH)
    sorted_spec = jnp.take(spectra, chan_order, axis=2)
    sorted_spec = sorted_spec.reshape(spectra.shape[0], 2, chan_count, block_width, FB)
    sorted_spec = jnp.moveaxis(sorted_spec, 2, 0)
    pieces = []
    for distance in range(chan_count):
        target = jnp.mod(chan_position + distance, chan_count)
        piece = lax.dynamic_index_in_dim(sorted_spec, target, 0, keepdims=False)
        pieces.append(piece if distance == 0 else shifted(piece, "chan", distance))
    own = jnp.stack(pieces)
    offsets = [max(1, round_index * chan_count // 4) for round_index in range(ROUNDS)]

    def send_slices(group):
        piece = lax.dynamic_slice_in_dim(group, tm_position * slice_width, slice_width, axis=4)
        return [shifted(piece, "chan", offset) for offset in offsets]

    gathered = own[None]
    partner_groups = [send_slices(gathered)]
    step = tm_count // 2
    while step >= 1:
        route = [(q, q ^ step) for q in range(tm_count)]
        arrived = lax.ppermute(gathered, "tm", route)
        partner_groups.append(send_slices(arrived))
        gathered = jnp.concatenate([gathered, arrived], axis=0)
        step //= 2
    early = 2 if gathered.shape[0] > 2 else gathered.shape[0]
    groups = [(0, early), (early, gathered.shape[0])] if early < gathered.shape[0] else [(0, early)]

    def own_operand(lo, hi):
        part = gathered[lo:hi]
        width = 2 * part.shape[0] * part.shape[1] * part.shape[2]
        return jnp.transpose(part, (5, 3, 0, 1, 2, 4)).reshape(FB, width, block_width)

    own_ops = [own_operand(lo, hi) for lo, hi in groups]
    inverse = inverse_table()
    results = []
    for round_index in range(ROUNDS):
        offset = offsets[round_index]
        partner = jnp.concatenate([group[round_index] for group in partner_groups], axis=0)
        partner = jnp.roll(partner, offset, axis=1)
        sums = None
        for (lo, hi), own_op in zip(groups, own_ops):
            part = partner[lo:hi]
            rotated = jnp.stack([-part[:, :, :, 1], part[:, :, :, 0]], axis=3)
            both = jnp.stack([part, rotated])
            both = jnp.transpose(both, (6, 0, 5, 4, 1, 2, 3)).reshape(FB, 2 * slice_width, own_op.shape[1])
            term = jnp.einsum("fnk,fkj->fnj", both, own_op, preferred_element_type=jnp.float32)
            sums = term if sums is None else sums + term
        sums = sums.reshape(FB, 2, slice_width, block_width)
        results.append(
            jnp.einsum("fcij,cfl->jil", sums, inverse, precision=lax.Precision.HIGH)
        )
    return jnp.stack(results)


def on_device(records, chan_order, live_mask):
    samples = records.shape[1]
    channels = records.shape[2]
    chan_count = lax.axis_size("chan")
    tm_count = lax.axis_size("tm")
    local_ok = (
        samples % L == 0
        and channels % chan_count == 0
        and (channels // chan_count) % tm_count == 0
        and (samples // L) * chan_count == WIN_TM
    )
    if local_ok:
        return on_device_local(records, chan_order, live_mask)
    return on_device_reduce(records, chan_order, live_mask)


def solution(mesh):
    placed = (P("tm", "chan", None), P(), P())
    return jax.shard_map(
        on_device,
        mesh=mesh,
        in_specs=placed,
        out_specs=P(None, "chan", "tm", None),
        check_vma=False,
    )
```

```python
import math

import jax
import jax.numpy as jnp
from jax import lax
from jax.sharding import PartitionSpec as P


L = 200
FB = 101
NLAG = 128
ROUNDS = 2
WIN_TM = 16


def shifted(block, axis, distance):
    devices = range(lax.axis_size(axis))
    route = [((i - distance) % len(devices), i) for i in devices]
    return lax.ppermute(block, axis, route)


def forward_table():
    sample_index = jnp.arange(L, dtype=jnp.int32)
    freq_index = jnp.arange(FB, dtype=jnp.int32)
    phase_step = jnp.mod(sample_index[:, None] * freq_index[None, :], L)
    phase_angle = phase_step.astype(jnp.float32) * (2.0 * math.pi / L)
    return jnp.concatenate([jnp.cos(phase_angle), -jnp.sin(phase_angle)], axis=1)


def smoothing_table():
    freq_index = jnp.arange(FB, dtype=jnp.int32)
    nearby = (jnp.abs(freq_index[:, None] - freq_index[None, :]) <= 2).astype(jnp.float32)
    return nearby / jnp.sum(nearby, axis=0, keepdims=True)


def inverse_table():
    freq_index = jnp.arange(FB, dtype=jnp.int32)
    lag_index = jnp.arange(NLAG, dtype=jnp.int32) - NLAG // 2
    phase_step = jnp.mod(freq_index[:, None] * lag_index[None, :], L)
    phase_angle = phase_step.astype(jnp.float32) * (2.0 * math.pi / L)
    edge = (freq_index == 0) | (freq_index == L // 2)
    fold_weight = jnp.where(edge, 1.0, 2.0).astype(jnp.float32) / L
    return jnp.stack(
        [fold_weight[:, None] * jnp.cos(phase_angle), -fold_weight[:, None] * jnp.sin(phase_angle)]
    )


def whiten_spectra(windows, live_block, precision=lax.Precision.HIGHEST):
    window_mean = jnp.mean(windows, axis=-2, keepdims=True)
    centred = windows - window_mean
    normed = centred / jnp.sqrt(jnp.mean(centred * centred, axis=-2, keepdims=True) + 1e-05)
    spectrum = jnp.einsum("...lk,lg->...kg", normed, forward_table(), precision=precision)
    real_part = spectrum[..., :FB]
    imag_part = spectrum[..., FB:]
    power = real_part * real_part + imag_part * imag_part
    smoothed = jnp.einsum("...f,fg->...g", power, smoothing_table(), precision=precision)
    mean_power = jnp.mean(power, axis=-1, keepdims=True)
    scale = live_block.astype(jnp.float32)[:, None] / jnp.sqrt(smoothed + 0.1 * mean_power + 1e-05)
    return jnp.concatenate([real_part * scale, imag_part * scale], axis=-1).astype(jnp.bfloat16)


def correlate(partner, own_spec, inverse):
    partner = partner.reshape(partner.shape[0], partner.shape[1], 2, FB)
    own_spec = own_spec.reshape(own_spec.shape[0], own_spec.shape[1], 2, FB)
    rotated = jnp.concatenate([own_spec[:, :, 1:2], -own_spec[:, :, 0:1]], axis=2)
    real_sum = jnp.einsum("wicf,wjcf->fji", partner, own_spec, preferred_element_type=jnp.float32)
    imag_sum = jnp.einsum("wicf,wjcf->fji", partner, rotated, preferred_element_type=jnp.float32)
    return jnp.einsum(
        "cfji,cfl->jil", jnp.stack([real_sum, imag_sum]), inverse, precision=lax.Precision.HIGHEST
    )


def on_device_reduce(records, chan_order, live_mask):
    chan_count = lax.axis_size("chan")
    position = lax.axis_index("chan")
    blocked = jnp.take(records, chan_order, axis=2)
    own_block = lax.all_to_all(blocked, "chan", split_axis=2, concat_axis=1, tiled=True)
    block_width = own_block.shape[2]
    own_windows = own_block.reshape(WIN_TM, L, block_width)
    live_blocks = jnp.take(live_mask, chan_order).reshape(chan_count, block_width)
    own_live = lax.dynamic_index_in_dim(live_blocks, position, 0, keepdims=False)
    own_spectra = whiten_spectra(own_windows, own_live)
    inverse = inverse_table()
    results = []
    for round_index in range(ROUNDS):
        offset = max(1, round_index * chan_count // 4)
        partner_block = shifted(own_windows, "chan", offset)
        source = jnp.mod(position - offset, chan_count)
        partner_live = lax.dynamic_index_in_dim(live_blocks, source, 0, keepdims=False)
        partner = whiten_spectra(partner_block, partner_live)
        lagged = correlate(partner, own_spectra, inverse)
        lagged = lax.psum_scatter(lagged, "tm", scatter_dimension=1, tiled=True)
        results.append(lagged)
    return jnp.stack(results)


def whiten_planes(windows, live, precision):
    window_mean = jnp.mean(windows, axis=-2, keepdims=True)
    centred = windows - window_mean
    normed = centred / jnp.sqrt(jnp.mean(centred * centred, axis=-2, keepdims=True) + 1e-05)
    table = forward_table()
    real_part = jnp.einsum("wlk,lg->wkg", normed, table[:, :FB], precision=precision)
    imag_part = jnp.einsum("wlk,lg->wkg", normed, table[:, FB:], precision=precision)
    power = real_part * real_part + imag_part * imag_part
    smoothed = jnp.einsum("wkf,fg->wkg", power, smoothing_table(), precision=precision)
    mean_power = jnp.mean(power, axis=-1, keepdims=True)
    scale = live.astype(jnp.float32)[:, None] / jnp.sqrt(smoothed + 0.1 * mean_power + 1e-05)
    return jnp.stack([real_part * scale, imag_part * scale], axis=1).astype(jnp.bfloat16)


def on_device_local(records, chan_order, live_mask):
    chan_count = lax.axis_size("chan")
    tm_count = lax.axis_size("tm")
    chan_position = lax.axis_index("chan")
    tm_position = lax.axis_index("tm")
    samples, channels = records.shape[1], records.shape[2]
    block_width = channels // chan_count
    slice_width = block_width // tm_count
    windows = records.reshape(samples // L, L, channels)
    spectra = whiten_planes(windows, live_mask, lax.Precision.HIGH)
    picks = (chan_order[:, None] == jnp.arange(channels, dtype=chan_order.dtype)[None, :])
    sorted_spec = jnp.einsum(
        "kh,wchf->wckf", picks.astype(jnp.bfloat16), spectra, preferred_element_type=jnp.float32
    ).astype(jnp.bfloat16)
    sorted_spec = sorted_spec.reshape(spectra.shape[0], 2, chan_count, block_width, FB)
    sorted_spec = jnp.moveaxis(sorted_spec, 2, 0)
    pieces = []
    for distance in range(chan_count):
        target = jnp.mod(chan_position + distance, chan_count)
        piece = lax.dynamic_index_in_dim(sorted_spec, target, 0, keepdims=False)
        pieces.append(piece if distance == 0 else shifted(piece, "chan", distance))
    own = jnp.stack(pieces)
    offsets = [max(1, round_index * chan_count // 4) for round_index in range(ROUNDS)]

    def send_slices(group):
        piece = lax.dynamic_slice_in_dim(group, tm_position * slice_width, slice_width, axis=4)
        return [shifted(piece, "chan", offset) for offset in offsets]

    gathered = own[None]
    partner_groups = [send_slices(gathered)]
    step = tm_count // 2
    while step >= 1:
        route = [(q, q ^ step) for q in range(tm_count)]
        arrived = lax.ppermute(gathered, "tm", route)
        partner_groups.append(send_slices(arrived))
        gathered = jnp.concatenate([gathered, arrived], axis=0)
        step //= 2
    windows_all = gathered.shape[0] * gathered.shape[1] * gathered.shape[2]
    own_spec = jnp.transpose(gathered, (5, 3, 0, 1, 2, 4)).reshape(FB, 2 * windows_all, block_width)
    inverse = inverse_table()
    results = []
    for round_index in range(ROUNDS):
        offset = max(1, round_index * chan_count // 4)
        partner_block = shifted(own_windows, "chan", offset)
        source = jnp.mod(position - offset, chan_count)
        partner_live = lax.dynamic_index_in_dim(live_blocks, source, 0, keepdims=False)
        partner = whiten_spectra(partner_block, partner_live)
        lagged = correlate(partner, own_spectra, inverse)
        lagged = lax.psum_scatter(lagged, "tm", scatter_dimension=1, tiled=True)
        results.append(lagged)
    return jnp.stack(results)


def whiten_planes(windows, live, precision):
    window_mean = jnp.mean(windows, axis=-2, keepdims=True)
    centred = windows - window_mean
    normed = centred / jnp.sqrt(jnp.mean(centred * centred, axis=-2, keepdims=True) + 1e-05)
    table = forward_table()
    real_part = jnp.einsum("wlk,lg->wkg", normed, table[:, :FB], precision=precision)
    imag_part = jnp.einsum("wlk,lg->wkg", normed, table[:, FB:], precision=precision)
    power = real_part * real_part + imag_part * imag_part
    smoothed = jnp.einsum("wkf,fg->wkg", power, smoothing_table(), precision=precision)
    mean_power = jnp.mean(power, axis=-1, keepdims=True)
    scale = live.astype(jnp.float32)[:, None] / jnp.sqrt(smoothed + 0.1 * mean_power + 1e-05)
    return jnp.stack([real_part * scale, imag_part * scale], axis=1).astype(jnp.bfloat16)


def on_device_local(records, chan_order, live_mask):
    chan_count = lax.axis_size("chan")
    tm_count = lax.axis_size("tm")
    chan_position = lax.axis_index("chan")
    tm_position = lax.axis_index("tm")
    samples, channels = records.shape[1], records.shape[2]
    block_width = channels // chan_count
    slice_width = block_width // tm_count
    windows = records.reshape(samples // L, L, channels)
    spectra = whiten_planes(windows, live_mask, lax.Precision.HIGH)
    picks = (chan_order[:, None] == jnp.arange(channels, dtype=chan_order.dtype)[None, :])
    sorted_spec = jnp.einsum(
        "kh,wchf->wckf", picks.astype(jnp.bfloat16), spectra, preferred_element_type=jnp.float32
    ).astype(jnp.bfloat16)
    sorted_spec = sorted_spec.reshape(spectra.shape[0], 2, chan_count, block_width, FB)
    sorted_spec = jnp.moveaxis(sorted_spec, 2, 0)
    pieces = []
    for distance in range(chan_count):
        target = jnp.mod(chan_position + distance, chan_count)
        piece = lax.dynamic_index_in_dim(sorted_spec, target, 0, keepdims=False)
        pieces.append(piece if distance == 0 else shifted(piece, "chan", distance))
    own = jnp.stack(pieces)
    offsets = [max(1, round_index * chan_count // 4) for round_index in range(ROUNDS)]

    def send_slices(group):
        piece = lax.dynamic_slice_in_dim(group, tm_position * slice_width, slice_width, axis=4)
        return [shifted(piece, "chan", offset) for offset in offsets]

    gathered = own[None]
    partner_groups = [send_slices(gathered)]
    step = tm_count // 2
    while step >= 1:
        route = [(q, q ^ step) for q in range(tm_count)]
        arrived = lax.ppermute(gathered, "tm", route)
        partner_groups.append(send_slices(arrived))
        gathered = jnp.concatenate([gathered, arrived], axis=0)
        step //= 2
    windows_all = gathered.shape[0] * gathered.shape[1] * gathered.shape[2]
    own_spec = jnp.transpose(gathered, (5, 3, 0, 1, 2, 4)).reshape(FB, 2 * windows_all, block_width)
    inverse = inverse_table()
    results = []
    for round_index in range(ROUNDS):
        offset = offsets[round_index]
        partner = jnp.concatenate([group[round_index] for group in partner_groups], axis=0)
        partner = jnp.roll(partner, offset, axis=1)
        rotated = jnp.stack([-partner[:, :, :, 1], partner[:, :, :, 0]], axis=3)
        both = jnp.stack([partner, rotated])
        both = jnp.transpose(both, (6, 0, 5, 4, 1, 2, 3)).reshape(FB, 2 * slice_width, 2 * windows_all)
        sums = jnp.einsum("fnk,fkj->fnj", both, own_spec, preferred_element_type=jnp.float32)
        sums = sums.reshape(FB, 2, slice_width, block_width)
        results.append(
            jnp.einsum("fcij,cfl->jil", sums, inverse, precision=lax.Precision.HIGH)
        )
    return jnp.stack(results)


def on_device(records, chan_order, live_mask):
    samples = records.shape[1]
    channels = records.shape[2]
    chan_count = lax.axis_size("chan")
    tm_count = lax.axis_size("tm")
    local_ok = (
        samples % L == 0
        and channels % chan_count == 0
        and (channels // chan_count) % tm_count == 0
        and (samples // L) * chan_count == WIN_TM
    )
    if local_ok:
        return on_device_local(records, chan_order, live_mask)
    return on_device_reduce(records, chan_order, live_mask)


def solution(mesh):
    placed = (P("tm", "chan", None), P(), P())
    return jax.shard_map(
        on_device,
        mesh=mesh,
        in_specs=placed,
        out_specs=P(None, "chan", "tm", None),
        check_vma=False,
    )
```

```python
import math

import jax
import jax.numpy as jnp
from jax import lax
from jax.sharding import PartitionSpec as P


L = 200
FB = 101
NLAG = 128
ROUNDS = 2
WIN_TM = 16


def shifted(block, axis, distance):
    devices = range(lax.axis_size(axis))
    route = [((i - distance) % len(devices), i) for i in devices]
    return lax.ppermute(block, axis, route)


def forward_table():
    sample_index = jnp.arange(L, dtype=jnp.int32)
    freq_index = jnp.arange(FB, dtype=jnp.int32)
    phase_step = jnp.mod(sample_index[:, None] * freq_index[None, :], L)
    phase_angle = phase_step.astype(jnp.float32) * (2.0 * math.pi / L)
    return jnp.concatenate([jnp.cos(phase_angle), -jnp.sin(phase_angle)], axis=1)


def smoothing_table():
    freq_index = jnp.arange(FB, dtype=jnp.int32)
    nearby = (jnp.abs(freq_index[:, None] - freq_index[None, :]) <= 2).astype(jnp.float32)
    return nearby / jnp.sum(nearby, axis=0, keepdims=True)


def inverse_table():
    freq_index = jnp.arange(FB, dtype=jnp.int32)
    lag_index = jnp.arange(NLAG, dtype=jnp.int32) - NLAG // 2
    phase_step = jnp.mod(freq_index[:, None] * lag_index[None, :], L)
    phase_angle = phase_step.astype(jnp.float32) * (2.0 * math.pi / L)
    edge = (freq_index == 0) | (freq_index == L // 2)
    fold_weight = jnp.where(edge, 1.0, 2.0).astype(jnp.float32) / L
    return jnp.stack(
        [fold_weight[:, None] * jnp.cos(phase_angle), -fold_weight[:, None] * jnp.sin(phase_angle)]
    )


def whiten_spectra(windows, live_block, precision=lax.Precision.HIGHEST):
    window_mean = jnp.mean(windows, axis=-2, keepdims=True)
    centred = windows - window_mean
    normed = centred / jnp.sqrt(jnp.mean(centred * centred, axis=-2, keepdims=True) + 1e-05)
    spectrum = jnp.einsum("...lk,lg->...kg", normed, forward_table(), precision=precision)
    real_part = spectrum[..., :FB]
    imag_part = spectrum[..., FB:]
    power = real_part * real_part + imag_part * imag_part
    smoothed = jnp.einsum("...f,fg->...g", power, smoothing_table(), precision=precision)
    mean_power = jnp.mean(power, axis=-1, keepdims=True)
    scale = live_block.astype(jnp.float32)[:, None] / jnp.sqrt(smoothed + 0.1 * mean_power + 1e-05)
    return jnp.concatenate([real_part * scale, imag_part * scale], axis=-1).astype(jnp.bfloat16)


def correlate(partner, own_spec, inverse):
    partner = partner.reshape(partner.shape[0], partner.shape[1], 2, FB)
    own_spec = own_spec.reshape(own_spec.shape[0], own_spec.shape[1], 2, FB)
    rotated = jnp.concatenate([own_spec[:, :, 1:2], -own_spec[:, :, 0:1]], axis=2)
    real_sum = jnp.einsum("wicf,wjcf->fji", partner, own_spec, preferred_element_type=jnp.float32)
    imag_sum = jnp.einsum("wicf,wjcf->fji", partner, rotated, preferred_element_type=jnp.float32)
    return jnp.einsum(
        "cfji,cfl->jil", jnp.stack([real_sum, imag_sum]), inverse, precision=lax.Precision.HIGHEST
    )


def on_device_reduce(records, chan_order, live_mask):
    chan_count = lax.axis_size("chan")
    position = lax.axis_index("chan")
    blocked = jnp.take(records, chan_order, axis=2)
    own_block = lax.all_to_all(blocked, "chan", split_axis=2, concat_axis=1, tiled=True)
    block_width = own_block.shape[2]
    own_windows = own_block.reshape(WIN_TM, L, block_width)
    live_blocks = jnp.take(live_mask, chan_order).reshape(chan_count, block_width)
    own_live = lax.dynamic_index_in_dim(live_blocks, position, 0, keepdims=False)
    own_spectra = whiten_spectra(own_windows, own_live)
    inverse = inverse_table()
    results = []
    for round_index in range(ROUNDS):
        offset = max(1, round_index * chan_count // 4)
        partner_block = shifted(own_windows, "chan", offset)
        source = jnp.mod(position - offset, chan_count)
        partner_live = lax.dynamic_index_in_dim(live_blocks, source, 0, keepdims=False)
        partner = whiten_spectra(partner_block, partner_live)
        lagged = correlate(partner, own_spectra, inverse)
        lagged = lax.psum_scatter(lagged, "tm", scatter_dimension=1, tiled=True)
        results.append(lagged)
    return jnp.stack(results)


def whiten_planes(windows, live, precision):
    window_mean = jnp.mean(windows, axis=-2, keepdims=True)
    centred = windows - window_mean
    normed = centred / jnp.sqrt(jnp.mean(centred * centred, axis=-2, keepdims=True) + 1e-05)
    table = forward_table()
    real_part = jnp.einsum("wlk,lg->wkg", normed, table[:, :FB], precision=precision)
    imag_part = jnp.einsum("wlk,lg->wkg", normed, table[:, FB:], precision=precision)
    power = real_part * real_part + imag_part * imag_part
    smoothed = jnp.einsum("wkf,fg->wkg", power, smoothing_table(), precision=precision)
    mean_power = jnp.mean(power, axis=-1, keepdims=True)
    scale = live.astype(jnp.float32)[:, None] / jnp.sqrt(smoothed + 0.1 * mean_power + 1e-05)
    return jnp.stack([real_part * scale, imag_part * scale], axis=1).astype(jnp.bfloat16)


def on_device_local(records, chan_order, live_mask):
    chan_count = lax.axis_size("chan")
    tm_count = lax.axis_size("tm")
    chan_position = lax.axis_index("chan")
    tm_position = lax.axis_index("tm")
    samples, channels = records.shape[1], records.shape[2]
    block_width = channels // chan_count
    slice_width = block_width // tm_count
    windows = records.reshape(samples // L, L, channels)
    spectra = whiten_planes(windows, live_mask, lax.Precision.HIGH)
    picks = (chan_order[:, None] == jnp.arange(channels, dtype=chan_order.dtype)[None, :])
    sorted_spec = jnp.einsum(
        "kh,wchf->wckf", picks.astype(jnp.bfloat16), spectra, preferred_element_type=jnp.float32
    ).astype(jnp.bfloat16)
    sorted_spec = sorted_spec.reshape(spectra.shape[0], 2, chan_count, block_width, FB)
    sorted_spec = jnp.moveaxis(sorted_spec, 2, 0)
    pieces = []
    for distance in range(chan_count):
        target = jnp.mod(chan_position + distance, chan_count)
        piece = lax.dynamic_index_in_dim(sorted_spec, target, 0, keepdims=False)
        pieces.append(piece if distance == 0 else shifted(piece, "chan", distance))
    own = jnp.stack(pieces)
    offsets = [max(1, round_index * chan_count // 4) for round_index in range(ROUNDS)]

    def send_slices(group):
        piece = lax.dynamic_slice_in_dim(group, tm_position * slice_width, slice_width, axis=4)
        sent = []
        for offset in offsets:
            sent.append(shifted(piece, "chan", offset))
        return sent

    gathered = own[None]
    partner_groups = [send_slices(gathered)]
    step = tm_count // 2
    while step >= 1:
        route = [(q, q ^ step) for q in range(tm_count)]
        arrived = lax.ppermute(gathered, "tm", route)
        partner_groups.append(send_slices(arrived))
        gathered = jnp.concatenate([gathered, arrived], axis=0)
        step //= 2
    windows_all = gathered.shape[0] * gathered.shape[1] * gathered.shape[2]
    own_spec = jnp.transpose(gathered, (5, 3, 0, 1, 2, 4)).reshape(FB, 2 * windows_all, block_width)
    inverse = inverse_table()
    results = []
    for round_index in range(ROUNDS):
        offset = max(1, round_index * chan_count // 4)
        partner_block = shifted(own_windows, "chan", offset)
        source = jnp.mod(position - offset, chan_count)
        partner_live = lax.dynamic_index_in_dim(live_blocks, source, 0, keepdims=False)
        partner = whiten_spectra(partner_block, partner_live)
        lagged = correlate(partner, own_spectra, inverse)
        lagged = lax.psum_scatter(lagged, "tm", scatter_dimension=1, tiled=True)
        results.append(lagged)
    return jnp.stack(results)


def whiten_planes(windows, live, precision):
    window_mean = jnp.mean(windows, axis=-2, keepdims=True)
    centred = windows - window_mean
    normed = centred / jnp.sqrt(jnp.mean(centred * centred, axis=-2, keepdims=True) + 1e-05)
    table = forward_table()
    real_part = jnp.einsum("wlk,lg->wkg", normed, table[:, :FB], precision=precision)
    imag_part = jnp.einsum("wlk,lg->wkg", normed, table[:, FB:], precision=precision)
    power = real_part * real_part + imag_part * imag_part
    smoothed = jnp.einsum("wkf,fg->wkg", power, smoothing_table(), precision=precision)
    mean_power = jnp.mean(power, axis=-1, keepdims=True)
    scale = live.astype(jnp.float32)[:, None] / jnp.sqrt(smoothed + 0.1 * mean_power + 1e-05)
    return jnp.stack([real_part * scale, imag_part * scale], axis=1).astype(jnp.bfloat16)


def on_device_local(records, chan_order, live_mask):
    chan_count = lax.axis_size("chan")
    tm_count = lax.axis_size("tm")
    chan_position = lax.axis_index("chan")
    tm_position = lax.axis_index("tm")
    samples, channels = records.shape[1], records.shape[2]
    block_width = channels // chan_count
    slice_width = block_width // tm_count
    windows = records.reshape(samples // L, L, channels)
    spectra = whiten_planes(windows, live_mask, lax.Precision.HIGH)
    picks = (chan_order[:, None] == jnp.arange(channels, dtype=chan_order.dtype)[None, :])
    sorted_spec = jnp.einsum(
        "kh,wchf->wckf", picks.astype(jnp.bfloat16), spectra, preferred_element_type=jnp.float32
    ).astype(jnp.bfloat16)
    sorted_spec = sorted_spec.reshape(spectra.shape[0], 2, chan_count, block_width, FB)
    sorted_spec = jnp.moveaxis(sorted_spec, 2, 0)
    pieces = []
    for distance in range(chan_count):
        target = jnp.mod(chan_position + distance, chan_count)
        piece = lax.dynamic_index_in_dim(sorted_spec, target, 0, keepdims=False)
        pieces.append(piece if distance == 0 else shifted(piece, "chan", distance))
    own = jnp.stack(pieces)
    offsets = [max(1, round_index * chan_count // 4) for round_index in range(ROUNDS)]

    def send_slices(group):
        piece = lax.dynamic_slice_in_dim(group, tm_position * slice_width, slice_width, axis=4)
        sent = []
        for offset in offsets:
            sent.append(shifted(piece, "chan", offset))
        return sent

    gathered = own[None]
    partner_groups = [send_slices(gathered)]
    step = tm_count // 2
    while step >= 1:
        route = [(q, q ^ step) for q in range(tm_count)]
        arrived = lax.ppermute(gathered, "tm", route)
        partner_groups.append(send_slices(arrived))
        gathered = jnp.concatenate([gathered, arrived], axis=0)
        step //= 2
    windows_all = gathered.shape[0] * gathered.shape[1] * gathered.shape[2]
    own_spec = jnp.transpose(gathered, (5, 3, 0, 1, 2, 4)).reshape(FB, 2 * windows_all, block_width)
    inverse = inverse_table()
    results = []
    for round_index in range(ROUNDS):
        offset = offsets[round_index]
        partner = jnp.concatenate([group[round_index] for group in partner_groups], axis=0)
        partner = jnp.roll(partner, offset, axis=1)
        rotated = jnp.stack([-partner[:, :, :, 1], partner[:, :, :, 0]], axis=3)
        both = jnp.stack([partner, rotated])
        both = jnp.transpose(both, (6, 0, 5, 4, 1, 2, 3)).reshape(FB, 2 * slice_width, 2 * windows_all)
        sums = jnp.einsum("fnk,fkj->fnj", both, own_spec, preferred_element_type=jnp.float32)
        sums = sums.reshape(FB, 2, slice_width, block_width)
        results.append(
            jnp.einsum("fcij,cfl->jil", sums, inverse, precision=lax.Precision.HIGH)
        )
    return jnp.stack(results)


def on_device(records, chan_order, live_mask):
    samples = records.shape[1]
    channels = records.shape[2]
    chan_count = lax.axis_size("chan")
    tm_count = lax.axis_size("tm")
    local_ok = (
        samples % L == 0
        and channels % chan_count == 0
        and (channels // chan_count) % tm_count == 0
        and (samples // L) * chan_count == WIN_TM
    )
    if local_ok:
        return on_device_local(records, chan_order, live_mask)
    return on_device_reduce(records, chan_order, live_mask)


def solution(mesh):
    placed = (P("tm", "chan", None), P(), P())
    return jax.shard_map(
        on_device,
        mesh=mesh,
        in_specs=placed,
        out_specs=P(None, "chan", "tm", None),
        check_vma=False,
    )
```

```python
import math

import jax
import jax.numpy as jnp
from jax import lax
from jax.sharding import PartitionSpec as P


L = 200
FB = 101
NLAG = 128
ROUNDS = 2
WIN_TM = 16


def shifted(block, axis, distance):
    devices = range(lax.axis_size(axis))
    route = [((i - distance) % len(devices), i) for i in devices]
    return lax.ppermute(block, axis, route)


def forward_table():
    sample_index = jnp.arange(L, dtype=jnp.int32)
    freq_index = jnp.arange(FB, dtype=jnp.int32)
    phase_step = jnp.mod(sample_index[:, None] * freq_index[None, :], L)
    phase_angle = phase_step.astype(jnp.float32) * (2.0 * math.pi / L)
    return jnp.concatenate([jnp.cos(phase_angle), -jnp.sin(phase_angle)], axis=1)


def smoothing_table():
    freq_index = jnp.arange(FB, dtype=jnp.int32)
    nearby = (jnp.abs(freq_index[:, None] - freq_index[None, :]) <= 2).astype(jnp.float32)
    return nearby / jnp.sum(nearby, axis=0, keepdims=True)


def inverse_table():
    freq_index = jnp.arange(FB, dtype=jnp.int32)
    lag_index = jnp.arange(NLAG, dtype=jnp.int32) - NLAG // 2
    phase_step = jnp.mod(freq_index[:, None] * lag_index[None, :], L)
    phase_angle = phase_step.astype(jnp.float32) * (2.0 * math.pi / L)
    edge = (freq_index == 0) | (freq_index == L // 2)
    fold_weight = jnp.where(edge, 1.0, 2.0).astype(jnp.float32) / L
    return jnp.stack(
        [fold_weight[:, None] * jnp.cos(phase_angle), -fold_weight[:, None] * jnp.sin(phase_angle)]
    )


def whiten_spectra(windows, live_block, precision=lax.Precision.HIGHEST):
    window_mean = jnp.mean(windows, axis=-2, keepdims=True)
    centred = windows - window_mean
    normed = centred / jnp.sqrt(jnp.mean(centred * centred, axis=-2, keepdims=True) + 1e-05)
    spectrum = jnp.einsum("...lk,lg->...kg", normed, forward_table(), precision=precision)
    real_part = spectrum[..., :FB]
    imag_part = spectrum[..., FB:]
    power = real_part * real_part + imag_part * imag_part
    smoothed = jnp.einsum("...f,fg->...g", power, smoothing_table(), precision=precision)
    mean_power = jnp.mean(power, axis=-1, keepdims=True)
    scale = live_block.astype(jnp.float32)[:, None] / jnp.sqrt(smoothed + 0.1 * mean_power + 1e-05)
    return jnp.concatenate([real_part * scale, imag_part * scale], axis=-1).astype(jnp.bfloat16)


def correlate(partner, own_spec, inverse):
    partner = partner.reshape(partner.shape[0], partner.shape[1], 2, FB)
    own_spec = own_spec.reshape(own_spec.shape[0], own_spec.shape[1], 2, FB)
    rotated = jnp.concatenate([own_spec[:, :, 1:2], -own_spec[:, :, 0:1]], axis=2)
    real_sum = jnp.einsum("wicf,wjcf->fji", partner, own_spec, preferred_element_type=jnp.float32)
    imag_sum = jnp.einsum("wicf,wjcf->fji", partner, rotated, preferred_element_type=jnp.float32)
    return jnp.einsum(
        "cfji,cfl->jil", jnp.stack([real_sum, imag_sum]), inverse, precision=lax.Precision.HIGHEST
    )


def on_device_reduce(records, chan_order, live_mask):
    chan_count = lax.axis_size("chan")
    position = lax.axis_index("chan")
    blocked = jnp.take(records, chan_order, axis=2)
    own_block = lax.all_to_all(blocked, "chan", split_axis=2, concat_axis=1, tiled=True)
    block_width = own_block.shape[2]
    own_windows = own_block.reshape(WIN_TM, L, block_width)
    live_blocks = jnp.take(live_mask, chan_order).reshape(chan_count, block_width)
    own_live = lax.dynamic_index_in_dim(live_blocks, position, 0, keepdims=False)
    own_spectra = whiten_spectra(own_windows, own_live)
    inverse = inverse_table()
    results = []
    for round_index in range(ROUNDS):
        offset = max(1, round_index * chan_count // 4)
        partner_block = shifted(own_windows, "chan", offset)
        source = jnp.mod(position - offset, chan_count)
        partner_live = lax.dynamic_index_in_dim(live_blocks, source, 0, keepdims=False)
        partner = whiten_spectra(partner_block, partner_live)
        lagged = correlate(partner, own_spectra, inverse)
        lagged = lax.psum_scatter(lagged, "tm", scatter_dimension=1, tiled=True)
        results.append(lagged)
    return jnp.stack(results)


def whiten_planes(windows, live, precision):
    window_mean = jnp.mean(windows, axis=-2, keepdims=True)
    centred = windows - window_mean
    normed = centred / jnp.sqrt(jnp.mean(centred * centred, axis=-2, keepdims=True) + 1e-05)
    table = forward_table()
    real_part = jnp.einsum("wlk,lg->wkg", normed, table[:, :FB], precision=precision)
    imag_part = jnp.einsum("wlk,lg->wkg", normed, table[:, FB:], precision=precision)
    power = real_part * real_part + imag_part * imag_part
    smoothed = jnp.einsum("wkf,fg->wkg", power, smoothing_table(), precision=precision)
    mean_power = jnp.mean(power, axis=-1, keepdims=True)
    scale = live.astype(jnp.float32)[:, None] / jnp.sqrt(smoothed + 0.1 * mean_power + 1e-05)
    return jnp.stack([real_part * scale, imag_part * scale], axis=1).astype(jnp.bfloat16)


def on_device_local(records, chan_order, live_mask):
    chan_count = lax.axis_size("chan")
    tm_count = lax.axis_size("tm")
    chan_position = lax.axis_index("chan")
    tm_position = lax.axis_index("tm")
    samples, channels = records.shape[1], records.shape[2]
    block_width = channels // chan_count
    slice_width = block_width // tm_count
    windows = records.reshape(samples // L, L, channels)
    spectra = whiten_planes(windows, live_mask, lax.Precision.HIGH)
    picks = (chan_order[:, None] == jnp.arange(channels, dtype=chan_order.dtype)[None, :])
    sorted_spec = jnp.einsum(
        "kh,wchf->wckf", picks.astype(jnp.bfloat16), spectra, preferred_element_type=jnp.float32
    ).astype(jnp.bfloat16)
    sorted_spec = sorted_spec.reshape(spectra.shape[0], 2, chan_count, block_width, FB)
    sorted_spec = jnp.moveaxis(sorted_spec, 2, 0)
    if chan_count % 2 == 0 and chan_count > 2:
        outer = chan_count // 2
        outer_position, inner_position = chan_position // 2, chan_position % 2
        outer_index = jnp.arange(outer, dtype=jnp.int32)
        theirs = jnp.take(sorted_spec, outer_index * 2 + (1 - inner_position), axis=0)
        mine = jnp.take(sorted_spec, outer_index * 2 + inner_position, axis=0)
        arrived = lax.ppermute(theirs, "chan", [(i, i ^ 1) for i in range(chan_count)])
        held = jnp.stack([mine, arrived], axis=1)
        pieces = []
        for distance in range(outer):
            target = jnp.mod(outer_position + distance, outer)
            piece = lax.dynamic_index_in_dim(held, target, 0, keepdims=False)
            pieces.append(piece if distance == 0 else shifted(piece, "chan", 2 * distance))
        by_shift = jnp.stack(pieces).reshape((chan_count,) + held.shape[2:])
        source = jnp.arange(chan_count, dtype=jnp.int32)
        slot = jnp.mod(outer_position - source // 2, outer) * 2 + jnp.bitwise_xor(source % 2, inner_position)
        own = jnp.take(by_shift, slot, axis=0)
    else:
        pieces = []
        for distance in range(chan_count):
            target = jnp.mod(chan_position + distance, chan_count)
            piece = lax.dynamic_index_in_dim(sorted_spec, target, 0, keepdims=False)
            pieces.append(piece if distance == 0 else shifted(piece, "chan", distance))
        by_shift = jnp.stack(pieces)
        source = jnp.arange(chan_count, dtype=jnp.int32)
        own = jnp.take(by_shift, jnp.mod(chan_position - source, chan_count), axis=0)
    offsets = [max(1, round_index * chan_count // 4) for round_index in range(ROUNDS)]

    def send_slices(group):
        piece = lax.dynamic_slice_in_dim(group, tm_position * slice_width, slice_width, axis=4)
        return [shifted(piece, "chan", offset) for offset in offsets]

    gathered = own[None]
    partner_groups = [send_slices(gathered)]
    step = tm_count // 2
    while step >= 1:
        route = [(q, q ^ step) for q in range(tm_count)]
        arrived = lax.ppermute(gathered, "tm", route)
        partner_groups.append(send_slices(arrived))
        gathered = jnp.concatenate([gathered, arrived], axis=0)
        step //= 2
    windows_all = gathered.shape[0] * gathered.shape[1] * gathered.shape[2]
    own_spec = jnp.transpose(gathered, (5, 3, 0, 1, 2, 4)).reshape(FB, 2 * windows_all, block_width)
    inverse = inverse_table()
    results = []
    for round_index in range(ROUNDS):
        partner = jnp.concatenate([group[round_index] for group in partner_groups], axis=0)
        rotated = jnp.stack([-partner[:, :, :, 1], partner[:, :, :, 0]], axis=3)
        both = jnp.stack([partner, rotated])
        both = jnp.transpose(both, (6, 0, 5, 4, 1, 2, 3)).reshape(FB, 2 * slice_width, 2 * windows_all)
        sums = jnp.einsum("fnk,fkj->fnj", both, own_spec, preferred_element_type=jnp.float32)
        sums = sums.reshape(FB, 2, slice_width, block_width)
        results.append(
            jnp.einsum("fcij,cfl->jil", sums, inverse, precision=lax.Precision.HIGH)
        )
    return jnp.stack(results)


def on_device(records, chan_order, live_mask):
    samples = records.shape[1]
    channels = records.shape[2]
    chan_count = lax.axis_size("chan")
    tm_count = lax.axis_size("tm")
    local_ok = (
        samples % L == 0
        and channels % chan_count == 0
        and (channels // chan_count) % tm_count == 0
        and (samples // L) * chan_count == WIN_TM
    )
    if local_ok:
        return on_device_local(records, chan_order, live_mask)
    return on_device_reduce(records, chan_order, live_mask)


def solution(mesh):
    placed = (P("tm", "chan", None), P(), P())
    return jax.shard_map(
        on_device,
        mesh=mesh,
        in_specs=placed,
        out_specs=P(None, "chan", "tm", None),
        check_vma=False,
    )
```

```python
import math

import jax
import jax.numpy as jnp
from jax import lax
from jax.sharding import PartitionSpec as P


L = 200
FB = 101
NLAG = 128
ROUNDS = 2
WIN_TM = 16


def shifted(block, axis, distance):
    devices = range(lax.axis_size(axis))
    route = [((i - distance) % len(devices), i) for i in devices]
    return lax.ppermute(block, axis, route)


def forward_table():
    sample_index = jnp.arange(L, dtype=jnp.int32)
    freq_index = jnp.arange(FB, dtype=jnp.int32)
    phase_step = jnp.mod(sample_index[:, None] * freq_index[None, :], L)
    phase_angle = phase_step.astype(jnp.float32) * (2.0 * math.pi / L)
    return jnp.concatenate([jnp.cos(phase_angle), -jnp.sin(phase_angle)], axis=1)


def smoothing_table():
    freq_index = jnp.arange(FB, dtype=jnp.int32)
    nearby = (jnp.abs(freq_index[:, None] - freq_index[None, :]) <= 2).astype(jnp.float32)
    return nearby / jnp.sum(nearby, axis=0, keepdims=True)


def inverse_table():
    freq_index = jnp.arange(FB, dtype=jnp.int32)
    lag_index = jnp.arange(NLAG, dtype=jnp.int32) - NLAG // 2
    phase_step = jnp.mod(freq_index[:, None] * lag_index[None, :], L)
    phase_angle = phase_step.astype(jnp.float32) * (2.0 * math.pi / L)
    edge = (freq_index == 0) | (freq_index == L // 2)
    fold_weight = jnp.where(edge, 1.0, 2.0).astype(jnp.float32) / L
    return jnp.stack(
        [fold_weight[:, None] * jnp.cos(phase_angle), -fold_weight[:, None] * jnp.sin(phase_angle)]
    )


def whiten_spectra(windows, live_block, precision=lax.Precision.HIGHEST):
    window_mean = jnp.mean(windows, axis=-2, keepdims=True)
    centred = windows - window_mean
    normed = centred / jnp.sqrt(jnp.mean(centred * centred, axis=-2, keepdims=True) + 1e-05)
    spectrum = jnp.einsum("...lk,lg->...kg", normed, forward_table(), precision=precision)
    real_part = spectrum[..., :FB]
    imag_part = spectrum[..., FB:]
    power = real_part * real_part + imag_part * imag_part
    smoothed = jnp.einsum("...f,fg->...g", power, smoothing_table(), precision=precision)
    mean_power = jnp.mean(power, axis=-1, keepdims=True)
    scale = live_block.astype(jnp.float32)[:, None] / jnp.sqrt(smoothed + 0.1 * mean_power + 1e-05)
    return jnp.concatenate([real_part * scale, imag_part * scale], axis=-1).astype(jnp.bfloat16)


def correlate(partner, own_spec, inverse):
    partner = partner.reshape(partner.shape[0], partner.shape[1], 2, FB)
    own_spec = own_spec.reshape(own_spec.shape[0], own_spec.shape[1], 2, FB)
    rotated = jnp.concatenate([own_spec[:, :, 1:2], -own_spec[:, :, 0:1]], axis=2)
    real_sum = jnp.einsum("wicf,wjcf->fji", partner, own_spec, preferred_element_type=jnp.float32)
    imag_sum = jnp.einsum("wicf,wjcf->fji", partner, rotated, preferred_element_type=jnp.float32)
    return jnp.einsum(
        "cfji,cfl->jil", jnp.stack([real_sum, imag_sum]), inverse, precision=lax.Precision.HIGHEST
    )


def on_device_reduce(records, chan_order, live_mask):
    chan_count = lax.axis_size("chan")
    position = lax.axis_index("chan")
    blocked = jnp.take(records, chan_order, axis=2)
    own_block = lax.all_to_all(blocked, "chan", split_axis=2, concat_axis=1, tiled=True)
    block_width = own_block.shape[2]
    own_windows = own_block.reshape(WIN_TM, L, block_width)
    live_blocks = jnp.take(live_mask, chan_order).reshape(chan_count, block_width)
    own_live = lax.dynamic_index_in_dim(live_blocks, position, 0, keepdims=False)
    own_spectra = whiten_spectra(own_windows, own_live)
    inverse = inverse_table()
    results = []
    for round_index in range(ROUNDS):
        offset = max(1, round_index * chan_count // 4)
        partner_block = shifted(own_windows, "chan", offset)
        source = jnp.mod(position - offset, chan_count)
        partner_live = lax.dynamic_index_in_dim(live_blocks, source, 0, keepdims=False)
        partner = whiten_spectra(partner_block, partner_live)
        lagged = correlate(partner, own_spectra, inverse)
        lagged = lax.psum_scatter(lagged, "tm", scatter_dimension=1, tiled=True)
        results.append(lagged)
    return jnp.stack(results)


def whiten_planes(windows, live, precision):
    window_mean = jnp.mean(windows, axis=-2, keepdims=True)
    centred = windows - window_mean
    normed = centred / jnp.sqrt(jnp.mean(centred * centred, axis=-2, keepdims=True) + 1e-05)
    table = forward_table()
    real_part = jnp.einsum("wlk,lg->wkg", normed, table[:, :FB], precision=precision)
    imag_part = jnp.einsum("wlk,lg->wkg", normed, table[:, FB:], precision=precision)
    power = real_part * real_part + imag_part * imag_part
    smoothed = jnp.einsum("wkf,fg->wkg", power, smoothing_table(), precision=precision)
    mean_power = jnp.mean(power, axis=-1, keepdims=True)
    scale = live.astype(jnp.float32)[:, None] / jnp.sqrt(smoothed + 0.1 * mean_power + 1e-05)
    return jnp.stack([real_part * scale, imag_part * scale], axis=1).astype(jnp.bfloat16)


def on_device_local(records, chan_order, live_mask):
    chan_count = lax.axis_size("chan")
    tm_count = lax.axis_size("tm")
    chan_position = lax.axis_index("chan")
    tm_position = lax.axis_index("tm")
    samples, channels = records.shape[1], records.shape[2]
    block_width = channels // chan_count
    slice_width = block_width // tm_count
    windows = records.reshape(samples // L, L, channels)
    spectra = whiten_planes(windows, live_mask, lax.Precision.HIGH)
    picks = (chan_order[:, None] == jnp.arange(channels, dtype=chan_order.dtype)[None, :])
    sorted_spec = jnp.einsum(
        "kh,wchf->wckf", picks.astype(jnp.bfloat16), spectra, preferred_element_type=jnp.float32
    ).astype(jnp.bfloat16)
    sorted_spec = sorted_spec.reshape(spectra.shape[0], 2, chan_count, block_width, FB)
    sorted_spec = jnp.moveaxis(sorted_spec, 2, 0)
    pieces = []
    for distance in range(chan_count):
        target = jnp.mod(chan_position + distance, chan_count)
        piece = lax.dynamic_index_in_dim(sorted_spec, target, 0, keepdims=False)
        pieces.append(piece if distance == 0 else shifted(piece, "chan", distance))
    own = jnp.stack(pieces)
    offsets = [max(1, round_index * chan_count // 4) for round_index in range(ROUNDS)]

    def send_slices(group):
        piece = lax.dynamic_slice_in_dim(group, tm_position * slice_width, slice_width, axis=4)
        return [shifted(piece, "chan", offset) for offset in offsets]

    gathered = own[None]
    partner_groups = [send_slices(gathered)]
    step = tm_count // 2
    grid = [(c, q) for c in range(chan_count) for q in range(tm_count)]

    def send_from_neighbour(group, mask):
        piece = lax.dynamic_slice_in_dim(
            group, jnp.bitwise_xor(tm_position, mask) * slice_width, slice_width, axis=4
        )
        sent = []
        for offset in offsets:
            route = [
                (c * tm_count + q, ((c + offset) % chan_count) * tm_count + (q ^ mask))
                for c, q in grid
            ]
            sent.append(lax.ppermute(piece, ("chan", "tm"), route))
        return sent

    while step >= 1:
        route = [(q, q ^ step) for q in range(tm_count)]
        arrived = lax.ppermute(gathered, "tm", route)
        if step == 1:
            partner_groups.append(send_from_neighbour(gathered, step))
        else:
            partner_groups.append(send_slices(arrived))
        gathered = jnp.concatenate([gathered, arrived], axis=0)
        step //= 2
    windows_all = gathered.shape[0] * gathered.shape[1] * gathered.shape[2]
    own_spec = jnp.transpose(gathered, (5, 3, 0, 1, 2, 4)).reshape(FB, 2 * windows_all, block_width)
    inverse = inverse_table()
    results = []
    for round_index in range(ROUNDS):
        offset = offsets[round_index]
        partner = jnp.concatenate([group[round_index] for group in partner_groups], axis=0)
        partner = jnp.roll(partner, offset, axis=1)
        rotated = jnp.stack([-partner[:, :, :, 1], partner[:, :, :, 0]], axis=3)
        both = jnp.stack([partner, rotated])
        both = jnp.transpose(both, (6, 0, 5, 4, 1, 2, 3)).reshape(FB, 2 * slice_width, 2 * windows_all)
        sums = jnp.einsum("fnk,fkj->fnj", both, own_spec, preferred_element_type=jnp.float32)
        sums = sums.reshape(FB, 2, slice_width, block_width)
        results.append(
            jnp.einsum("fcij,cfl->jil", sums, inverse, precision=lax.Precision.HIGH)
        )
    return jnp.stack(results)


def on_device(records, chan_order, live_mask):
    samples = records.shape[1]
    channels = records.shape[2]
    chan_count = lax.axis_size("chan")
    tm_count = lax.axis_size("tm")
    local_ok = (
        samples % L == 0
        and channels % chan_count == 0
        and (channels // chan_count) % tm_count == 0
        and (samples // L) * chan_count == WIN_TM
    )
    if local_ok:
        return on_device_local(records, chan_order, live_mask)
    return on_device_reduce(records, chan_order, live_mask)


def solution(mesh):
    placed = (P("tm", "chan", None), P(), P())
    return jax.shard_map(
        on_device,
        mesh=mesh,
        in_specs=placed,
        out_specs=P(None, "chan", "tm", None),
        check_vma=False,
    )
```

```python
import math

import jax
import jax.numpy as jnp
from jax import lax
from jax.sharding import PartitionSpec as P


L = 200
FB = 101
NLAG = 128
ROUNDS = 2
WIN_TM = 16


def shifted(block, axis, distance):
    devices = range(lax.axis_size(axis))
    route = [((i - distance) % len(devices), i) for i in devices]
    return lax.ppermute(block, axis, route)


def forward_table():
    sample_index = jnp.arange(L, dtype=jnp.int32)
    freq_index = jnp.arange(FB, dtype=jnp.int32)
    phase_step = jnp.mod(sample_index[:, None] * freq_index[None, :], L)
    phase_angle = phase_step.astype(jnp.float32) * (2.0 * math.pi / L)
    return jnp.concatenate([jnp.cos(phase_angle), -jnp.sin(phase_angle)], axis=1)


def smoothing_table():
    freq_index = jnp.arange(FB, dtype=jnp.int32)
    nearby = (jnp.abs(freq_index[:, None] - freq_index[None, :]) <= 2).astype(jnp.float32)
    return nearby / jnp.sum(nearby, axis=0, keepdims=True)


def inverse_table():
    freq_index = jnp.arange(FB, dtype=jnp.int32)
    lag_index = jnp.arange(NLAG, dtype=jnp.int32) - NLAG // 2
    phase_step = jnp.mod(freq_index[:, None] * lag_index[None, :], L)
    phase_angle = phase_step.astype(jnp.float32) * (2.0 * math.pi / L)
    edge = (freq_index == 0) | (freq_index == L // 2)
    fold_weight = jnp.where(edge, 1.0, 2.0).astype(jnp.float32) / L
    return jnp.stack(
        [fold_weight[:, None] * jnp.cos(phase_angle), -fold_weight[:, None] * jnp.sin(phase_angle)]
    )


def whiten_spectra(windows, live_block, precision=lax.Precision.HIGHEST):
    window_mean = jnp.mean(windows, axis=-2, keepdims=True)
    centred = windows - window_mean
    normed = centred / jnp.sqrt(jnp.mean(centred * centred, axis=-2, keepdims=True) + 1e-05)
    spectrum = jnp.einsum("...lk,lg->...kg", normed, forward_table(), precision=precision)
    real_part = spectrum[..., :FB]
    imag_part = spectrum[..., FB:]
    power = real_part * real_part + imag_part * imag_part
    smoothed = jnp.einsum("...f,fg->...g", power, smoothing_table(), precision=precision)
    mean_power = jnp.mean(power, axis=-1, keepdims=True)
    scale = live_block.astype(jnp.float32)[:, None] / jnp.sqrt(smoothed + 0.1 * mean_power + 1e-05)
    return jnp.concatenate([real_part * scale, imag_part * scale], axis=-1).astype(jnp.bfloat16)


def correlate(partner, own_spec, inverse):
    partner = partner.reshape(partner.shape[0], partner.shape[1], 2, FB)
    own_spec = own_spec.reshape(own_spec.shape[0], own_spec.shape[1], 2, FB)
    rotated = jnp.concatenate([own_spec[:, :, 1:2], -own_spec[:, :, 0:1]], axis=2)
    real_sum = jnp.einsum("wicf,wjcf->fji", partner, own_spec, preferred_element_type=jnp.float32)
    imag_sum = jnp.einsum("wicf,wjcf->fji", partner, rotated, preferred_element_type=jnp.float32)
    return jnp.einsum(
        "cfji,cfl->jil", jnp.stack([real_sum, imag_sum]), inverse, precision=lax.Precision.HIGHEST
    )


def on_device_reduce(records, chan_order, live_mask):
    chan_count = lax.axis_size("chan")
    position = lax.axis_index("chan")
    blocked = jnp.take(records, chan_order, axis=2)
    own_block = lax.all_to_all(blocked, "chan", split_axis=2, concat_axis=1, tiled=True)
    block_width = own_block.shape[2]
    own_windows = own_block.reshape(WIN_TM, L, block_width)
    live_blocks = jnp.take(live_mask, chan_order).reshape(chan_count, block_width)
    own_live = lax.dynamic_index_in_dim(live_blocks, position, 0, keepdims=False)
    own_spectra = whiten_spectra(own_windows, own_live)
    inverse = inverse_table()
    results = []
    for round_index in range(ROUNDS):
        offset = max(1, round_index * chan_count // 4)
        partner_block = shifted(own_windows, "chan", offset)
        source = jnp.mod(position - offset, chan_count)
        partner_live = lax.dynamic_index_in_dim(live_blocks, source, 0, keepdims=False)
        partner = whiten_spectra(partner_block, partner_live)
        lagged = correlate(partner, own_spectra, inverse)
        lagged = lax.psum_scatter(lagged, "tm", scatter_dimension=1, tiled=True)
        results.append(lagged)
    return jnp.stack(results)


def whiten_planes(windows, live, precision):
    window_mean = jnp.mean(windows, axis=-2, keepdims=True)
    centred = windows - window_mean
    normed = centred / jnp.sqrt(jnp.mean(centred * centred, axis=-2, keepdims=True) + 1e-05)
    table = forward_table()
    real_part = jnp.einsum("wlk,lg->wkg", normed, table[:, :FB], precision=precision)
    imag_part = jnp.einsum("wlk,lg->wkg", normed, table[:, FB:], precision=precision)
    power = real_part * real_part + imag_part * imag_part
    smoothed = jnp.einsum("wkf,fg->wkg", power, smoothing_table(), precision=precision)
    mean_power = jnp.mean(power, axis=-1, keepdims=True)
    scale = live.astype(jnp.float32)[:, None] / jnp.sqrt(smoothed + 0.1 * mean_power + 1e-05)
    return jnp.stack([real_part * scale, imag_part * scale], axis=1).astype(jnp.bfloat16)


def on_device_local(records, chan_order, live_mask):
    chan_count = lax.axis_size("chan")
    tm_count = lax.axis_size("tm")
    chan_position = lax.axis_index("chan")
    tm_position = lax.axis_index("tm")
    samples, channels = records.shape[1], records.shape[2]
    block_width = channels // chan_count
    slice_width = block_width // tm_count
    windows = records.reshape(samples // L, L, channels)
    spectra = whiten_planes(windows, live_mask, lax.Precision.HIGH)
    picks = (chan_order[:, None] == jnp.arange(channels, dtype=chan_order.dtype)[None, :])
    sorted_spec = jnp.einsum(
        "kh,wchf->wckf", picks.astype(jnp.bfloat16), spectra, preferred_element_type=jnp.float32
    ).astype(jnp.bfloat16)
    sorted_spec = sorted_spec.reshape(spectra.shape[0], 2, chan_count, block_width, FB)
    sorted_spec = jnp.moveaxis(sorted_spec, 2, 0)
    pieces = []
    for distance in range(chan_count):
        target = jnp.mod(chan_position + distance, chan_count)
        piece = lax.dynamic_index_in_dim(sorted_spec, target, 0, keepdims=False)
        pieces.append(piece if distance == 0 else shifted(piece, "chan", distance))
    by_shift = jnp.stack(pieces)
    source = jnp.arange(chan_count, dtype=jnp.int32)
    own = jnp.take(by_shift, jnp.mod(chan_position - source, chan_count), axis=0)
    offsets = [max(1, round_index * chan_count // 4) for round_index in range(ROUNDS)]

    def send_slices(group):
        piece = lax.dynamic_slice_in_dim(group, tm_position * slice_width, slice_width, axis=4)
        return [shifted(piece, "chan", offset) for offset in offsets]

    grid = [(c, q) for c in range(chan_count) for q in range(tm_count)]

    def send_from_neighbour(group, mask):
        piece = lax.dynamic_slice_in_dim(
            group, jnp.bitwise_xor(tm_position, mask) * slice_width, slice_width, axis=4
        )
        sent = []
        for offset in offsets:
            route = [
                (c * tm_count + q, ((c + offset) % chan_count) * tm_count + (q ^ mask))
                for c, q in grid
            ]
            sent.append(lax.ppermute(piece, ("chan", "tm"), route))
        return sent

    gathered = own[None]
    if tm_count == 4:
        slot0 = send_slices(gathered)
        slot2 = send_from_neighbour(gathered, 1)
        arrived = lax.ppermute(gathered, "tm", [(q, q ^ 2) for q in range(tm_count)])
        slot1 = send_slices(arrived)
        slot3 = send_from_neighbour(arrived, 1)
        gathered = jnp.concatenate([gathered, arrived], axis=0)
        arrived = lax.ppermute(gathered, "tm", [(q, q ^ 1) for q in range(tm_count)])
        own_groups = [gathered, arrived]
        partner_sets = [[slot0, slot1], [slot2, slot3]]
    else:
        partner_groups = [send_slices(gathered)]
        step = tm_count // 2
        while step >= 1:
            route = [(q, q ^ step) for q in range(tm_count)]
            arrived = lax.ppermute(gathered, "tm", route)
            partner_groups.append(send_slices(arrived))
            gathered = jnp.concatenate([gathered, arrived], axis=0)
            step //= 2
        own_groups = [gathered]
        partner_sets = [partner_groups]
    own_specs = []
    for group in own_groups:
        width = 2 * group.shape[0] * group.shape[1] * group.shape[2]
        own_specs.append(jnp.transpose(group, (5, 3, 0, 1, 2, 4)).reshape(FB, width, block_width))
    inverse = inverse_table()
    results = []
    for round_index in range(ROUNDS):
        sums = None
        for pieces_of_half, own_spec in zip(partner_sets, own_specs):
            partner = jnp.concatenate([piece[round_index] for piece in pieces_of_half], axis=0)
            rotated = jnp.stack([-partner[:, :, :, 1], partner[:, :, :, 0]], axis=3)
            both = jnp.stack([partner, rotated])
            both = jnp.transpose(both, (6, 0, 5, 4, 1, 2, 3)).reshape(FB, 2 * slice_width, own_spec.shape[1])
            term = jnp.einsum("fnk,fkj->fnj", both, own_spec, preferred_element_type=jnp.float32)
            sums = term if sums is None else sums + term
        sums = sums.reshape(FB, 2, slice_width, block_width)
        results.append(
            jnp.einsum("fcij,cfl->jil", sums, inverse, precision=lax.Precision.HIGH)
        )
    return jnp.stack(results)


def on_device(records, chan_order, live_mask):
    samples = records.shape[1]
    channels = records.shape[2]
    chan_count = lax.axis_size("chan")
    tm_count = lax.axis_size("tm")
    local_ok = (
        samples % L == 0
        and channels % chan_count == 0
        and (channels // chan_count) % tm_count == 0
        and (samples // L) * chan_count == WIN_TM
    )
    if local_ok:
        return on_device_local(records, chan_order, live_mask)
    return on_device_reduce(records, chan_order, live_mask)


def solution(mesh):
    placed = (P("tm", "chan", None), P(), P())
    return jax.shard_map(
        on_device,
        mesh=mesh,
        in_specs=placed,
        out_specs=P(None, "chan", "tm", None),
        check_vma=False,
    )
```

```python
import math

import jax
import jax.numpy as jnp
from jax import lax
from jax.sharding import PartitionSpec as P


L = 200
FB = 101
NLAG = 128
ROUNDS = 2
WIN_TM = 16


def shifted(block, axis, distance):
    devices = range(lax.axis_size(axis))
    route = [((i - distance) % len(devices), i) for i in devices]
    return lax.ppermute(block, axis, route)


def forward_table():
    sample_index = jnp.arange(L, dtype=jnp.int32)
    freq_index = jnp.arange(FB, dtype=jnp.int32)
    phase_step = jnp.mod(sample_index[:, None] * freq_index[None, :], L)
    phase_angle = phase_step.astype(jnp.float32) * (2.0 * math.pi / L)
    return jnp.concatenate([jnp.cos(phase_angle), -jnp.sin(phase_angle)], axis=1)


def smoothing_table():
    freq_index = jnp.arange(FB, dtype=jnp.int32)
    nearby = (jnp.abs(freq_index[:, None] - freq_index[None, :]) <= 2).astype(jnp.float32)
    return nearby / jnp.sum(nearby, axis=0, keepdims=True)


def inverse_table():
    freq_index = jnp.arange(FB, dtype=jnp.int32)
    lag_index = jnp.arange(NLAG, dtype=jnp.int32) - NLAG // 2
    phase_step = jnp.mod(freq_index[:, None] * lag_index[None, :], L)
    phase_angle = phase_step.astype(jnp.float32) * (2.0 * math.pi / L)
    edge = (freq_index == 0) | (freq_index == L // 2)
    fold_weight = jnp.where(edge, 1.0, 2.0).astype(jnp.float32) / L
    return jnp.stack(
        [fold_weight[:, None] * jnp.cos(phase_angle), -fold_weight[:, None] * jnp.sin(phase_angle)]
    )


def whiten_spectra(windows, live_block, precision=lax.Precision.HIGHEST):
    window_mean = jnp.mean(windows, axis=-2, keepdims=True)
    centred = windows - window_mean
    normed = centred / jnp.sqrt(jnp.mean(centred * centred, axis=-2, keepdims=True) + 1e-05)
    spectrum = jnp.einsum("...lk,lg->...kg", normed, forward_table(), precision=precision)
    real_part = spectrum[..., :FB]
    imag_part = spectrum[..., FB:]
    power = real_part * real_part + imag_part * imag_part
    smoothed = jnp.einsum("...f,fg->...g", power, smoothing_table(), precision=precision)
    mean_power = jnp.mean(power, axis=-1, keepdims=True)
    scale = live_block.astype(jnp.float32)[:, None] / jnp.sqrt(smoothed + 0.1 * mean_power + 1e-05)
    return jnp.concatenate([real_part * scale, imag_part * scale], axis=-1).astype(jnp.bfloat16)


def correlate(partner, own_spec, inverse):
    partner = partner.reshape(partner.shape[0], partner.shape[1], 2, FB)
    own_spec = own_spec.reshape(own_spec.shape[0], own_spec.shape[1], 2, FB)
    rotated = jnp.concatenate([own_spec[:, :, 1:2], -own_spec[:, :, 0:1]], axis=2)
    real_sum = jnp.einsum("wicf,wjcf->fji", partner, own_spec, preferred_element_type=jnp.float32)
    imag_sum = jnp.einsum("wicf,wjcf->fji", partner, rotated, preferred_element_type=jnp.float32)
    return jnp.einsum(
        "cfji,cfl->jil", jnp.stack([real_sum, imag_sum]), inverse, precision=lax.Precision.HIGHEST
    )


def on_device_reduce(records, chan_order, live_mask):
    chan_count = lax.axis_size("chan")
    position = lax.axis_index("chan")
    blocked = jnp.take(records, chan_order, axis=2)
    own_block = lax.all_to_all(blocked, "chan", split_axis=2, concat_axis=1, tiled=True)
    block_width = own_block.shape[2]
    own_windows = own_block.reshape(WIN_TM, L, block_width)
    live_blocks = jnp.take(live_mask, chan_order).reshape(chan_count, block_width)
    own_live = lax.dynamic_index_in_dim(live_blocks, position, 0, keepdims=False)
    own_spectra = whiten_spectra(own_windows, own_live)
    inverse = inverse_table()
    results = []
    for round_index in range(ROUNDS):
        offset = max(1, round_index * chan_count // 4)
        partner_block = shifted(own_windows, "chan", offset)
        source = jnp.mod(position - offset, chan_count)
        partner_live = lax.dynamic_index_in_dim(live_blocks, source, 0, keepdims=False)
        partner = whiten_spectra(partner_block, partner_live)
        lagged = correlate(partner, own_spectra, inverse)
        lagged = lax.psum_scatter(lagged, "tm", scatter_dimension=1, tiled=True)
        results.append(lagged)
    return jnp.stack(results)


def whiten_planes(windows, live, precision):
    window_mean = jnp.mean(windows, axis=-2, keepdims=True)
    centred = windows - window_mean
    normed = centred / jnp.sqrt(jnp.mean(centred * centred, axis=-2, keepdims=True) + 1e-05)
    table = forward_table()
    real_part = jnp.einsum("wlk,lg->wkg", normed, table[:, :FB], precision=precision)
    imag_part = jnp.einsum("wlk,lg->wkg", normed, table[:, FB:], precision=precision)
    power = real_part * real_part + imag_part * imag_part
    smoothed = jnp.einsum("wkf,fg->wkg", power, smoothing_table(), precision=precision)
    mean_power = jnp.mean(power, axis=-1, keepdims=True)
    scale = live.astype(jnp.float32)[:, None] / jnp.sqrt(smoothed + 0.1 * mean_power + 1e-05)
    return jnp.stack([real_part * scale, imag_part * scale], axis=1).astype(jnp.bfloat16)


def on_device_local(records, chan_order, live_mask):
    chan_count = lax.axis_size("chan")
    tm_count = lax.axis_size("tm")
    chan_position = lax.axis_index("chan")
    tm_position = lax.axis_index("tm")
    samples, channels = records.shape[1], records.shape[2]
    block_width = channels // chan_count
    slice_width = block_width // tm_count
    windows = records.reshape(samples // L, L, channels)
    spectra = whiten_planes(windows, live_mask, lax.Precision.HIGH)
    picks = (chan_order[:, None] == jnp.arange(channels, dtype=chan_order.dtype)[None, :])
    sorted_spec = jnp.einsum(
        "kh,wchf->wckf", picks.astype(jnp.bfloat16), spectra, preferred_element_type=jnp.float32
    ).astype(jnp.bfloat16)
    sorted_spec = sorted_spec.reshape(spectra.shape[0], 2, chan_count, block_width, FB)
    sorted_spec = jnp.moveaxis(sorted_spec, 2, 0)
    pieces = []
    for distance in range(chan_count):
        target = jnp.mod(chan_position + distance, chan_count)
        piece = lax.dynamic_index_in_dim(sorted_spec, target, 0, keepdims=False)
        pieces.append(piece if distance == 0 else shifted(piece, "chan", distance))
    own = jnp.stack(pieces)
    offsets = [max(1, round_index * chan_count // 4) for round_index in range(ROUNDS)]

    def send_slices(group):
        piece = lax.dynamic_slice_in_dim(group, tm_position * slice_width, slice_width, axis=4)
        return [shifted(piece, "chan", offset) for offset in offsets]

    grid = [(c, q) for c in range(chan_count) for q in range(tm_count)]

    def send_from_neighbour(group, mask):
        piece = lax.dynamic_slice_in_dim(
            group, jnp.bitwise_xor(tm_position, mask) * slice_width, slice_width, axis=4
        )
        sent = []
        for offset in offsets:
            route = [
                (c * tm_count + q, ((c + offset) % chan_count) * tm_count + (q ^ mask))
                for c, q in grid
            ]
            sent.append(lax.ppermute(piece, ("chan", "tm"), route))
        return sent

    gathered = own[None]
    if tm_count == 4:
        slot0 = send_slices(gathered)
        slot2 = send_from_neighbour(gathered, 1)
        arrived = lax.ppermute(gathered, "tm", [(q, q ^ 2) for q in range(tm_count)])
        slot1 = send_slices(arrived)
        slot3 = send_from_neighbour(arrived, 1)
        gathered = jnp.concatenate([gathered, arrived], axis=0)
        arrived = lax.ppermute(gathered, "tm", [(q, q ^ 1) for q in range(tm_count)])
        gathered = jnp.concatenate([gathered, arrived], axis=0)
        partner_groups = [slot0, slot1, slot2, slot3]
    else:
        partner_groups = [send_slices(gathered)]
        step = tm_count // 2
        while step >= 1:
            route = [(q, q ^ step) for q in range(tm_count)]
            arrived = lax.ppermute(gathered, "tm", route)
            partner_groups.append(send_slices(arrived))
            gathered = jnp.concatenate([gathered, arrived], axis=0)
            step //= 2
    windows_all = gathered.shape[0] * gathered.shape[1] * gathered.shape[2]
    own_spec = jnp.transpose(gathered, (5, 3, 0, 1, 2, 4)).reshape(FB, 2 * windows_all, block_width)
    inverse = inverse_table()
    results = []
    for round_index in range(ROUNDS):
        offset = offsets[round_index]
        partner = jnp.concatenate([group[round_index] for group in partner_groups], axis=0)
        partner = jnp.roll(partner, offset, axis=1)
        rotated = jnp.stack([-partner[:, :, :, 1], partner[:, :, :, 0]], axis=3)
        both = jnp.stack([partner, rotated])
        both = jnp.transpose(both, (6, 0, 5, 4, 1, 2, 3)).reshape(FB, 2 * slice_width, 2 * windows_all)
        sums = jnp.einsum("fnk,fkj->fnj", both, own_spec, preferred_element_type=jnp.float32)
        sums = sums.reshape(FB, 2, slice_width, block_width)
        results.append(
            jnp.einsum("fcij,cfl->jil", sums, inverse, precision=lax.Precision.DEFAULT)
        )
    return jnp.stack(results)


def on_device(records, chan_order, live_mask):
    samples = records.shape[1]
    channels = records.shape[2]
    chan_count = lax.axis_size("chan")
    tm_count = lax.axis_size("tm")
    local_ok = (
        samples % L == 0
        and channels % chan_count == 0
        and (channels // chan_count) % tm_count == 0
        and (samples // L) * chan_count == WIN_TM
    )
    if local_ok:
        return on_device_local(records, chan_order, live_mask)
    return on_device_reduce(records, chan_order, live_mask)


def solution(mesh):
    placed = (P("tm", "chan", None), P(), P())
    return jax.shard_map(
        on_device,
        mesh=mesh,
        in_specs=placed,
        out_specs=P(None, "chan", "tm", None),
        check_vma=False,
    )
```

```python
import math

import jax
import jax.numpy as jnp
from jax import lax
from jax.sharding import PartitionSpec as P


L = 200
FB = 101
NLAG = 128
ROUNDS = 2
WIN_TM = 16


def shifted(block, axis, distance):
    devices = range(lax.axis_size(axis))
    route = [((i - distance) % len(devices), i) for i in devices]
    return lax.ppermute(block, axis, route)


def forward_table():
    sample_index = jnp.arange(L, dtype=jnp.int32)
    freq_index = jnp.arange(FB, dtype=jnp.int32)
    phase_step = jnp.mod(sample_index[:, None] * freq_index[None, :], L)
    phase_angle = phase_step.astype(jnp.float32) * (2.0 * math.pi / L)
    return jnp.concatenate([jnp.cos(phase_angle), -jnp.sin(phase_angle)], axis=1)


def smoothing_table():
    freq_index = jnp.arange(FB, dtype=jnp.int32)
    nearby = (jnp.abs(freq_index[:, None] - freq_index[None, :]) <= 2).astype(jnp.float32)
    return nearby / jnp.sum(nearby, axis=0, keepdims=True)


def inverse_table():
    freq_index = jnp.arange(FB, dtype=jnp.int32)
    lag_index = jnp.arange(NLAG, dtype=jnp.int32) - NLAG // 2
    phase_step = jnp.mod(freq_index[:, None] * lag_index[None, :], L)
    phase_angle = phase_step.astype(jnp.float32) * (2.0 * math.pi / L)
    edge = (freq_index == 0) | (freq_index == L // 2)
    fold_weight = jnp.where(edge, 1.0, 2.0).astype(jnp.float32) / L
    return jnp.stack(
        [fold_weight[:, None] * jnp.cos(phase_angle), -fold_weight[:, None] * jnp.sin(phase_angle)]
    )


def whiten_spectra(windows, live_block, precision=lax.Precision.HIGHEST):
    window_mean = jnp.mean(windows, axis=-2, keepdims=True)
    centred = windows - window_mean
    normed = centred / jnp.sqrt(jnp.mean(centred * centred, axis=-2, keepdims=True) + 1e-05)
    spectrum = jnp.einsum("...lk,lg->...kg", normed, forward_table(), precision=precision)
    real_part = spectrum[..., :FB]
    imag_part = spectrum[..., FB:]
    power = real_part * real_part + imag_part * imag_part
    smoothed = jnp.einsum("...f,fg->...g", power, smoothing_table(), precision=precision)
    mean_power = jnp.mean(power, axis=-1, keepdims=True)
    scale = live_block.astype(jnp.float32)[:, None] / jnp.sqrt(smoothed + 0.1 * mean_power + 1e-05)
    return jnp.concatenate([real_part * scale, imag_part * scale], axis=-1).astype(jnp.bfloat16)


def correlate(partner, own_spec, inverse):
    partner = partner.reshape(partner.shape[0], partner.shape[1], 2, FB)
    own_spec = own_spec.reshape(own_spec.shape[0], own_spec.shape[1], 2, FB)
    rotated = jnp.concatenate([own_spec[:, :, 1:2], -own_spec[:, :, 0:1]], axis=2)
    real_sum = jnp.einsum("wicf,wjcf->fji", partner, own_spec, preferred_element_type=jnp.float32)
    imag_sum = jnp.einsum("wicf,wjcf->fji", partner, rotated, preferred_element_type=jnp.float32)
    return jnp.einsum(
        "cfji,cfl->jil", jnp.stack([real_sum, imag_sum]), inverse, precision=lax.Precision.HIGHEST
    )


def on_device_reduce(records, chan_order, live_mask):
    chan_count = lax.axis_size("chan")
    position = lax.axis_index("chan")
    blocked = jnp.take(records, chan_order, axis=2)
    own_block = lax.all_to_all(blocked, "chan", split_axis=2, concat_axis=1, tiled=True)
    block_width = own_block.shape[2]
    own_windows = own_block.reshape(WIN_TM, L, block_width)
    live_blocks = jnp.take(live_mask, chan_order).reshape(chan_count, block_width)
    own_live = lax.dynamic_index_in_dim(live_blocks, position, 0, keepdims=False)
    own_spectra = whiten_spectra(own_windows, own_live)
    inverse = inverse_table()
    results = []
    for round_index in range(ROUNDS):
        offset = max(1, round_index * chan_count // 4)
        partner_block = shifted(own_windows, "chan", offset)
        source = jnp.mod(position - offset, chan_count)
        partner_live = lax.dynamic_index_in_dim(live_blocks, source, 0, keepdims=False)
        partner = whiten_spectra(partner_block, partner_live)
        lagged = correlate(partner, own_spectra, inverse)
        lagged = lax.psum_scatter(lagged, "tm", scatter_dimension=1, tiled=True)
        results.append(lagged)
    return jnp.stack(results)


def whiten_planes(windows, live, precision):
    window_mean = jnp.mean(windows, axis=-2, keepdims=True)
    centred = windows - window_mean
    normed = centred / jnp.sqrt(jnp.mean(centred * centred, axis=-2, keepdims=True) + 1e-05)
    table = forward_table()
    real_part = jnp.einsum("wlk,lg->wkg", normed, table[:, :FB], precision=precision)
    imag_part = jnp.einsum("wlk,lg->wkg", normed, table[:, FB:], precision=precision)
    power = real_part * real_part + imag_part * imag_part
    smoothed = jnp.einsum("wkf,fg->wkg", power, smoothing_table(), precision=precision)
    mean_power = jnp.mean(power, axis=-1, keepdims=True)
    scale = live.astype(jnp.float32)[:, None] / jnp.sqrt(smoothed + 0.1 * mean_power + 1e-05)
    return jnp.stack([real_part * scale, imag_part * scale], axis=1).astype(jnp.bfloat16)


def on_device_local(records, chan_order, live_mask):
    chan_count = lax.axis_size("chan")
    tm_count = lax.axis_size("tm")
    chan_position = lax.axis_index("chan")
    tm_position = lax.axis_index("tm")
    samples, channels = records.shape[1], records.shape[2]
    block_width = channels // chan_count
    slice_width = block_width // tm_count
    windows = records.reshape(samples // L, L, channels)
    spectra = whiten_planes(windows, live_mask, lax.Precision.HIGH)
    picks = (chan_order[:, None] == jnp.arange(channels, dtype=chan_order.dtype)[None, :])
    sorted_spec = jnp.einsum(
        "kh,wchf->wckf", picks.astype(jnp.bfloat16), spectra, preferred_element_type=jnp.float32
    ).astype(jnp.bfloat16)
    sorted_spec = sorted_spec.reshape(spectra.shape[0], 2, chan_count, block_width, FB)
    sorted_spec = jnp.moveaxis(sorted_spec, 2, 0)
    pieces = []
    for distance in range(chan_count):
        target = jnp.mod(chan_position + distance, chan_count)
        piece = lax.dynamic_index_in_dim(sorted_spec, target, 0, keepdims=False)
        if distance == 0:
            pieces.append(piece)
        else:
            pieces.append(shifted(piece, "chan", distance))
    own = jnp.stack(pieces)
    offsets = [max(1, round_index * chan_count // 4) for round_index in range(ROUNDS)]

    def send_slices(group):
        piece = lax.dynamic_slice_in_dim(group, tm_position * slice_width, slice_width, axis=4)
        return [shifted(piece, "chan", offset) for offset in offsets]

    grid = [(c, q) for c in range(chan_count) for q in range(tm_count)]

    def send_from_neighbour(group, mask):
        piece = lax.dynamic_slice_in_dim(
            group, jnp.bitwise_xor(tm_position, mask) * slice_width, slice_width, axis=4
        )
        sent = []
        for offset in offsets:
            route = [
                (c * tm_count + q, ((c + offset) % chan_count) * tm_count + (q ^ mask))
                for c, q in grid
            ]
            sent.append(lax.ppermute(piece, ("chan", "tm"), route))
        return sent

    gathered = own[None]
    if tm_count == 4:
        slot0 = send_slices(gathered)
        slot2 = send_from_neighbour(gathered, 1)
        arrived = lax.ppermute(gathered, "tm", [(q, q ^ 2) for q in range(tm_count)])
        slot1 = send_slices(arrived)
        slot3 = send_from_neighbour(arrived, 1)
        gathered = jnp.concatenate([gathered, arrived], axis=0)
        arrived = lax.ppermute(gathered, "tm", [(q, q ^ 1) for q in range(tm_count)])
        gathered = jnp.concatenate([gathered, arrived], axis=0)
        partner_groups = [slot0, slot1, slot2, slot3]
    else:
        partner_groups = [send_slices(gathered)]
        step = tm_count // 2
        while step >= 1:
            route = [(q, q ^ step) for q in range(tm_count)]
            arrived = lax.ppermute(gathered, "tm", route)
            partner_groups.append(send_slices(arrived))
            gathered = jnp.concatenate([gathered, arrived], axis=0)
            step //= 2
    windows_all = gathered.shape[0] * gathered.shape[1] * gathered.shape[2]
    own_spec = jnp.transpose(gathered, (5, 3, 0, 1, 2, 4)).reshape(FB, 2 * windows_all, block_width)
    inverse = inverse_table()
    results = []
    for round_index in range(ROUNDS):
        offset = offsets[round_index]
        partner = jnp.concatenate([group[round_index] for group in partner_groups], axis=0)
        partner = jnp.roll(partner, offset, axis=1)
        rotated = jnp.stack([-partner[:, :, :, 1], partner[:, :, :, 0]], axis=3)
        both = jnp.stack([partner, rotated])
        both = jnp.transpose(both, (6, 0, 5, 4, 1, 2, 3)).reshape(FB, 2 * slice_width, 2 * windows_all)
        sums = jnp.einsum("fnk,fkj->fnj", both, own_spec, preferred_element_type=jnp.float32)
        sums = sums.reshape(FB, 2, slice_width, block_width)
        results.append(
            jnp.einsum("fcij,cfl->jil", sums, inverse, precision=lax.Precision.HIGH)
        )
    return jnp.stack(results)


def on_device(records, chan_order, live_mask):
    samples = records.shape[1]
    channels = records.shape[2]
    chan_count = lax.axis_size("chan")
    tm_count = lax.axis_size("tm")
    local_ok = (
        samples % L == 0
        and channels % chan_count == 0
        and (channels // chan_count) % tm_count == 0
        and (samples // L) * chan_count == WIN_TM
    )
    if local_ok:
        return on_device_local(records, chan_order, live_mask)
    return on_device_reduce(records, chan_order, live_mask)


def solution(mesh):
    placed = (P("tm", "chan", None), P(), P())
    return jax.shard_map(
        on_device,
        mesh=mesh,
        in_specs=placed,
        out_specs=P(None, "chan", "tm", None),
        check_vma=False,
    )
```

```python
import math

import jax
import jax.numpy as jnp
from jax import lax
from jax.sharding import PartitionSpec as P


L = 200
FB = 101
NLAG = 128
ROUNDS = 2
WIN_TM = 16


def shifted(block, axis, distance):
    devices = range(lax.axis_size(axis))
    route = [((i - distance) % len(devices), i) for i in devices]
    return lax.ppermute(block, axis, route)


def forward_table():
    sample_index = jnp.arange(L, dtype=jnp.int32)
    freq_index = jnp.arange(FB, dtype=jnp.int32)
    phase_step = jnp.mod(sample_index[:, None] * freq_index[None, :], L)
    phase_angle = phase_step.astype(jnp.float32) * (2.0 * math.pi / L)
    return jnp.concatenate([jnp.cos(phase_angle), -jnp.sin(phase_angle)], axis=1)


def smoothing_table():
    freq_index = jnp.arange(FB, dtype=jnp.int32)
    nearby = (jnp.abs(freq_index[:, None] - freq_index[None, :]) <= 2).astype(jnp.float32)
    return nearby / jnp.sum(nearby, axis=0, keepdims=True)


def inverse_table():
    freq_index = jnp.arange(FB, dtype=jnp.int32)
    lag_index = jnp.arange(NLAG, dtype=jnp.int32) - NLAG // 2
    phase_step = jnp.mod(freq_index[:, None] * lag_index[None, :], L)
    phase_angle = phase_step.astype(jnp.float32) * (2.0 * math.pi / L)
    edge = (freq_index == 0) | (freq_index == L // 2)
    fold_weight = jnp.where(edge, 1.0, 2.0).astype(jnp.float32) / L
    return jnp.stack(
        [fold_weight[:, None] * jnp.cos(phase_angle), -fold_weight[:, None] * jnp.sin(phase_angle)]
    )


def whiten_spectra(windows, live_block, precision=lax.Precision.HIGHEST):
    window_mean = jnp.mean(windows, axis=-2, keepdims=True)
    centred = windows - window_mean
    normed = centred / jnp.sqrt(jnp.mean(centred * centred, axis=-2, keepdims=True) + 1e-05)
    spectrum = jnp.einsum("...lk,lg->...kg", normed, forward_table(), precision=precision)
    real_part = spectrum[..., :FB]
    imag_part = spectrum[..., FB:]
    power = real_part * real_part + imag_part * imag_part
    smoothed = jnp.einsum("...f,fg->...g", power, smoothing_table(), precision=precision)
    mean_power = jnp.mean(power, axis=-1, keepdims=True)
    scale = live_block.astype(jnp.float32)[:, None] / jnp.sqrt(smoothed + 0.1 * mean_power + 1e-05)
    return jnp.concatenate([real_part * scale, imag_part * scale], axis=-1).astype(jnp.bfloat16)


def correlate(partner, own_spec, inverse):
    partner = partner.reshape(partner.shape[0], partner.shape[1], 2, FB)
    own_spec = own_spec.reshape(own_spec.shape[0], own_spec.shape[1], 2, FB)
    rotated = jnp.concatenate([own_spec[:, :, 1:2], -own_spec[:, :, 0:1]], axis=2)
    real_sum = jnp.einsum("wicf,wjcf->fji", partner, own_spec, preferred_element_type=jnp.float32)
    imag_sum = jnp.einsum("wicf,wjcf->fji", partner, rotated, preferred_element_type=jnp.float32)
    return jnp.einsum(
        "cfji,cfl->jil", jnp.stack([real_sum, imag_sum]), inverse, precision=lax.Precision.HIGHEST
    )


def on_device_reduce(records, chan_order, live_mask):
    chan_count = lax.axis_size("chan")
    position = lax.axis_index("chan")
    blocked = jnp.take(records, chan_order, axis=2)
    own_block = lax.all_to_all(blocked, "chan", split_axis=2, concat_axis=1, tiled=True)
    block_width = own_block.shape[2]
    own_windows = own_block.reshape(WIN_TM, L, block_width)
    live_blocks = jnp.take(live_mask, chan_order).reshape(chan_count, block_width)
    own_live = lax.dynamic_index_in_dim(live_blocks, position, 0, keepdims=False)
    own_spectra = whiten_spectra(own_windows, own_live)
    inverse = inverse_table()
    results = []
    for round_index in range(ROUNDS):
        offset = max(1, round_index * chan_count // 4)
        partner_block = shifted(own_windows, "chan", offset)
        source = jnp.mod(position - offset, chan_count)
        partner_live = lax.dynamic_index_in_dim(live_blocks, source, 0, keepdims=False)
        partner = whiten_spectra(partner_block, partner_live)
        lagged = correlate(partner, own_spectra, inverse)
        lagged = lax.psum_scatter(lagged, "tm", scatter_dimension=1, tiled=True)
        results.append(lagged)
    return jnp.stack(results)


def whiten_planes(windows, live, precision):
    window_mean = jnp.mean(windows, axis=-2, keepdims=True)
    centred = windows - window_mean
    normed = centred / jnp.sqrt(jnp.mean(centred * centred, axis=-2, keepdims=True) + 1e-05)
    table = forward_table()
    real_part = jnp.einsum("wlk,lg->wkg", normed, table[:, :FB], precision=precision)
    imag_part = jnp.einsum("wlk,lg->wkg", normed, table[:, FB:], precision=precision)
    power = real_part * real_part + imag_part * imag_part
    smoothed = jnp.einsum("wkf,fg->wkg", power, smoothing_table(), precision=precision)
    mean_power = jnp.mean(power, axis=-1, keepdims=True)
    scale = live.astype(jnp.float32)[:, None] / jnp.sqrt(smoothed + 0.1 * mean_power + 1e-05)
    return jnp.stack([real_part * scale, imag_part * scale], axis=1).astype(jnp.bfloat16)


def on_device_local(records, chan_order, live_mask):
    chan_count = lax.axis_size("chan")
    tm_count = lax.axis_size("tm")
    chan_position = lax.axis_index("chan")
    tm_position = lax.axis_index("tm")
    samples, channels = records.shape[1], records.shape[2]
    block_width = channels // chan_count
    slice_width = block_width // tm_count
    windows = records.reshape(samples // L, L, channels)
    spectra = whiten_planes(windows, live_mask, lax.Precision.HIGH)
    picks = (chan_order[:, None] == jnp.arange(channels, dtype=chan_order.dtype)[None, :])
    sorted_spec = jnp.einsum(
        "kh,wchf->wckf", picks.astype(jnp.bfloat16), spectra, preferred_element_type=jnp.float32
    ).astype(jnp.bfloat16)
    sorted_spec = sorted_spec.reshape(spectra.shape[0], 2, chan_count, block_width, FB)
    sorted_spec = jnp.moveaxis(sorted_spec, 2, 0)
    pieces = []
    for distance in range(chan_count):
        target = jnp.mod(chan_position + distance, chan_count)
        piece = lax.dynamic_index_in_dim(sorted_spec, target, 0, keepdims=False)
        pieces.append(piece if distance == 0 else shifted(piece, "chan", distance))
    own = jnp.stack(pieces)
    offsets = [max(1, round_index * chan_count // 4) for round_index in range(ROUNDS)]

    def send_slices(group):
        piece = lax.dynamic_slice_in_dim(group, tm_position * slice_width, slice_width, axis=4)
        return [shifted(piece, "chan", offset) for offset in offsets]

    grid = [(c, q) for c in range(chan_count) for q in range(tm_count)]

    def send_from_neighbour(group, mask):
        piece = lax.dynamic_slice_in_dim(
            group, jnp.bitwise_xor(tm_position, mask) * slice_width, slice_width, axis=4
        )
        sent = []
        for offset in offsets:
            route = [
                (c * tm_count + q, ((c + offset) % chan_count) * tm_count + (q ^ mask))
                for c, q in grid
            ]
            sent.append(lax.ppermute(piece, ("chan", "tm"), route))
        return sent

    gathered = own[None]
    if tm_count == 4:
        slot0 = send_slices(gathered)
        slot2 = send_from_neighbour(gathered, 1)
        arrived = lax.ppermute(gathered, "tm", [(q, q ^ 2) for q in range(tm_count)])
        slot1 = send_slices(arrived)
        slot3 = send_from_neighbour(arrived, 1)
        gathered = jnp.concatenate([gathered, arrived], axis=0)
        arrived = lax.ppermute(gathered, "tm", [(q, q ^ 1) for q in range(tm_count)])
        gathered = jnp.concatenate([gathered, arrived], axis=0)
        partner_groups = [slot0, slot1, slot2, slot3]
    else:
        partner_groups = [send_slices(gathered)]
        step = tm_count // 2
        while step >= 1:
            route = [(q, q ^ step) for q in range(tm_count)]
            arrived = lax.ppermute(gathered, "tm", route)
            partner_groups.append(send_slices(arrived))
            gathered = jnp.concatenate([gathered, arrived], axis=0)
            step //= 2
    windows_all = gathered.shape[0] * gathered.shape[1] * gathered.shape[2]
    own_spec = jnp.transpose(gathered, (5, 3, 0, 1, 2, 4)).reshape(FB, 2 * windows_all, block_width)
    inverse = inverse_table()
    results = []
    for round_index in range(ROUNDS):
        offset = offsets[round_index]
        partner = jnp.concatenate([group[round_index] for group in partner_groups], axis=0)
        partner = jnp.roll(partner, offset, axis=1)
        rotated = jnp.stack([-partner[:, :, :, 1], partner[:, :, :, 0]], axis=3)
        both = jnp.stack([partner, rotated])
        both = jnp.transpose(both, (6, 0, 5, 4, 1, 2, 3)).reshape(FB, 2 * slice_width, 2 * windows_all)
        sums = jnp.einsum("fnk,fkj->fnj", both, own_spec, preferred_element_type=jnp.float32)
        results.append(sums.reshape(FB, 2, slice_width, block_width))
    sums = jnp.stack(results, axis=2)
    return jnp.einsum("fcrij,cfl->rjil", sums, inverse, precision=lax.Precision.HIGH)


def on_device(records, chan_order, live_mask):
    samples = records.shape[1]
    channels = records.shape[2]
    chan_count = lax.axis_size("chan")
    tm_count = lax.axis_size("tm")
    local_ok = (
        samples % L == 0
        and channels % chan_count == 0
        and (channels // chan_count) % tm_count == 0
        and (samples // L) * chan_count == WIN_TM
    )
    if local_ok:
        return on_device_local(records, chan_order, live_mask)
    return on_device_reduce(records, chan_order, live_mask)


def solution(mesh):
    placed = (P("tm", "chan", None), P(), P())
    return jax.shard_map(
        on_device,
        mesh=mesh,
        in_specs=placed,
        out_specs=P(None, "chan", "tm", None),
        check_vma=False,
    )
```

```python
import math

import jax
import jax.numpy as jnp
from jax import lax
from jax.sharding import PartitionSpec as P


L = 200
FB = 101
NLAG = 128
ROUNDS = 2
WIN_TM = 16


def shifted(block, axis, distance):
    devices = range(lax.axis_size(axis))
    route = [((i - distance) % len(devices), i) for i in devices]
    return lax.ppermute(block, axis, route)


def forward_table():
    sample_index = jnp.arange(L, dtype=jnp.int32)
    freq_index = jnp.arange(FB, dtype=jnp.int32)
    phase_step = jnp.mod(sample_index[:, None] * freq_index[None, :], L)
    phase_angle = phase_step.astype(jnp.float32) * (2.0 * math.pi / L)
    return jnp.concatenate([jnp.cos(phase_angle), -jnp.sin(phase_angle)], axis=1)


def smoothing_table():
    freq_index = jnp.arange(FB, dtype=jnp.int32)
    nearby = (jnp.abs(freq_index[:, None] - freq_index[None, :]) <= 2).astype(jnp.float32)
    return nearby / jnp.sum(nearby, axis=0, keepdims=True)


def inverse_table():
    freq_index = jnp.arange(FB, dtype=jnp.int32)
    lag_index = jnp.arange(NLAG, dtype=jnp.int32) - NLAG // 2
    phase_step = jnp.mod(freq_index[:, None] * lag_index[None, :], L)
    phase_angle = phase_step.astype(jnp.float32) * (2.0 * math.pi / L)
    edge = (freq_index == 0) | (freq_index == L // 2)
    fold_weight = jnp.where(edge, 1.0, 2.0).astype(jnp.float32) / L
    return jnp.stack(
        [fold_weight[:, None] * jnp.cos(phase_angle), -fold_weight[:, None] * jnp.sin(phase_angle)]
    )


def whiten_spectra(windows, live_block, precision=lax.Precision.HIGHEST):
    window_mean = jnp.mean(windows, axis=-2, keepdims=True)
    centred = windows - window_mean
    normed = centred / jnp.sqrt(jnp.mean(centred * centred, axis=-2, keepdims=True) + 1e-05)
    spectrum = jnp.einsum("...lk,lg->...kg", normed, forward_table(), precision=precision)
    real_part = spectrum[..., :FB]
    imag_part = spectrum[..., FB:]
    power = real_part * real_part + imag_part * imag_part
    smoothed = jnp.einsum("...f,fg->...g", power, smoothing_table(), precision=precision)
    mean_power = jnp.mean(power, axis=-1, keepdims=True)
    scale = live_block.astype(jnp.float32)[:, None] / jnp.sqrt(smoothed + 0.1 * mean_power + 1e-05)
    return jnp.concatenate([real_part * scale, imag_part * scale], axis=-1).astype(jnp.bfloat16)


def correlate(partner, own_spec, inverse):
    partner = partner.reshape(partner.shape[0], partner.shape[1], 2, FB)
    own_spec = own_spec.reshape(own_spec.shape[0], own_spec.shape[1], 2, FB)
    rotated = jnp.concatenate([own_spec[:, :, 1:2], -own_spec[:, :, 0:1]], axis=2)
    real_sum = jnp.einsum("wicf,wjcf->fji", partner, own_spec, preferred_element_type=jnp.float32)
    imag_sum = jnp.einsum("wicf,wjcf->fji", partner, rotated, preferred_element_type=jnp.float32)
    return jnp.einsum(
        "cfji,cfl->jil", jnp.stack([real_sum, imag_sum]), inverse, precision=lax.Precision.HIGHEST
    )


def on_device_reduce(records, chan_order, live_mask):
    chan_count = lax.axis_size("chan")
    position = lax.axis_index("chan")
    blocked = jnp.take(records, chan_order, axis=2)
    own_block = lax.all_to_all(blocked, "chan", split_axis=2, concat_axis=1, tiled=True)
    block_width = own_block.shape[2]
    own_windows = own_block.reshape(WIN_TM, L, block_width)
    live_blocks = jnp.take(live_mask, chan_order).reshape(chan_count, block_width)
    own_live = lax.dynamic_index_in_dim(live_blocks, position, 0, keepdims=False)
    own_spectra = whiten_spectra(own_windows, own_live)
    inverse = inverse_table()
    results = []
    for round_index in range(ROUNDS):
        offset = max(1, round_index * chan_count // 4)
        partner_block = shifted(own_windows, "chan", offset)
        source = jnp.mod(position - offset, chan_count)
        partner_live = lax.dynamic_index_in_dim(live_blocks, source, 0, keepdims=False)
        partner = whiten_spectra(partner_block, partner_live)
        lagged = correlate(partner, own_spectra, inverse)
        lagged = lax.psum_scatter(lagged, "tm", scatter_dimension=1, tiled=True)
        results.append(lagged)
    return jnp.stack(results)


def whiten_planes(windows, live, precision):
    window_mean = jnp.mean(windows, axis=-2, keepdims=True)
    centred = windows - window_mean
    normed = centred / jnp.sqrt(jnp.mean(centred * centred, axis=-2, keepdims=True) + 1e-05)
    table = forward_table()
    both_parts = jnp.einsum("wlk,lcg->wckg", normed, table.reshape(L, 2, FB), precision=precision)
    real_part, imag_part = both_parts[:, 0], both_parts[:, 1]
    power = real_part * real_part + imag_part * imag_part
    smoothed = jnp.einsum("wkf,fg->wkg", power, smoothing_table(), precision=precision)
    mean_power = jnp.mean(power, axis=-1, keepdims=True)
    scale = live.astype(jnp.float32)[:, None] / jnp.sqrt(smoothed + 0.1 * mean_power + 1e-05)
    return (both_parts * scale[:, None]).astype(jnp.bfloat16)


def on_device_local(records, chan_order, live_mask):
    chan_count = lax.axis_size("chan")
    tm_count = lax.axis_size("tm")
    chan_position = lax.axis_index("chan")
    tm_position = lax.axis_index("tm")
    samples, channels = records.shape[1], records.shape[2]
    block_width = channels // chan_count
    slice_width = block_width // tm_count
    windows = records.reshape(samples // L, L, channels)
    spectra = whiten_planes(windows, live_mask, lax.Precision.HIGH)
    picks = (chan_order[:, None] == jnp.arange(channels, dtype=chan_order.dtype)[None, :])
    sorted_spec = jnp.einsum(
        "kh,wchf->wckf", picks.astype(jnp.bfloat16), spectra, preferred_element_type=jnp.float32
    ).astype(jnp.bfloat16)
    sorted_spec = sorted_spec.reshape(spectra.shape[0], 2, chan_count, block_width, FB)
    sorted_spec = jnp.moveaxis(sorted_spec, 2, 0)
    pieces = []
    for distance in range(chan_count):
        target = jnp.mod(chan_position + distance, chan_count)
        piece = lax.dynamic_index_in_dim(sorted_spec, target, 0, keepdims=False)
        pieces.append(piece if distance == 0 else shifted(piece, "chan", distance))
    own = jnp.stack(pieces)
    offsets = [max(1, round_index * chan_count // 4) for round_index in range(ROUNDS)]

    def send_slices(group):
        piece = lax.dynamic_slice_in_dim(group, tm_position * slice_width, slice_width, axis=4)
        return [shifted(piece, "chan", offset) for offset in offsets]

    grid = [(c, q) for c in range(chan_count) for q in range(tm_count)]

    def send_from_neighbour(group, mask):
        piece = lax.dynamic_slice_in_dim(
            group, jnp.bitwise_xor(tm_position, mask) * slice_width, slice_width, axis=4
        )
        sent = []
        for offset in offsets:
            route = [
                (c * tm_count + q, ((c + offset) % chan_count) * tm_count + (q ^ mask))
                for c, q in grid
            ]
            sent.append(lax.ppermute(piece, ("chan", "tm"), route))
        return sent

    gathered = own[None]
    if tm_count == 4:
        slot0 = send_slices(gathered)
        slot2 = send_from_neighbour(gathered, 1)
        arrived = lax.ppermute(gathered, "tm", [(q, q ^ 2) for q in range(tm_count)])
        slot1 = send_slices(arrived)
        slot3 = send_from_neighbour(arrived, 1)
        gathered = jnp.concatenate([gathered, arrived], axis=0)
        arrived = lax.ppermute(gathered, "tm", [(q, q ^ 1) for q in range(tm_count)])
        gathered = jnp.concatenate([gathered, arrived], axis=0)
        partner_groups = [slot0, slot1, slot2, slot3]
    else:
        partner_groups = [send_slices(gathered)]
        step = tm_count // 2
        while step >= 1:
            route = [(q, q ^ step) for q in range(tm_count)]
            arrived = lax.ppermute(gathered, "tm", route)
            partner_groups.append(send_slices(arrived))
            gathered = jnp.concatenate([gathered, arrived], axis=0)
            step //= 2
    windows_all = gathered.shape[0] * gathered.shape[1] * gathered.shape[2]
    own_spec = jnp.transpose(gathered, (5, 3, 0, 1, 2, 4)).reshape(FB, 2 * windows_all, block_width)
    inverse = inverse_table()
    results = []
    for round_index in range(ROUNDS):
        offset = offsets[round_index]
        partner = jnp.concatenate([group[round_index] for group in partner_groups], axis=0)
        partner = jnp.roll(partner, offset, axis=1)
        rotated = jnp.stack([-partner[:, :, :, 1], partner[:, :, :, 0]], axis=3)
        both = jnp.stack([partner, rotated])
        both = jnp.transpose(both, (6, 0, 5, 4, 1, 2, 3)).reshape(FB, 2 * slice_width, 2 * windows_all)
        sums = jnp.einsum("fnk,fkj->fnj", both, own_spec, preferred_element_type=jnp.float32)
        sums = sums.reshape(FB, 2, slice_width, block_width)
        results.append(
            jnp.einsum("fcij,cfl->jil", sums, inverse, precision=lax.Precision.HIGH)
        )
    return jnp.stack(results)


def on_device(records, chan_order, live_mask):
    samples = records.shape[1]
    channels = records.shape[2]
    chan_count = lax.axis_size("chan")
    tm_count = lax.axis_size("tm")
    local_ok = (
        samples % L == 0
        and channels % chan_count == 0
        and (channels // chan_count) % tm_count == 0
        and (samples // L) * chan_count == WIN_TM
    )
    if local_ok:
        return on_device_local(records, chan_order, live_mask)
    return on_device_reduce(records, chan_order, live_mask)


def solution(mesh):
    placed = (P("tm", "chan", None), P(), P())
    return jax.shard_map(
        on_device,
        mesh=mesh,
        in_specs=placed,
        out_specs=P(None, "chan", "tm", None),
        check_vma=False,
    )
```
